256 devices in a mesh: sp: 64 (over y, z_lo, x), dp: 4 (over z_hi, core).
Axes of the slice: x: 4, y: 4, z: 8 (z_hi: 2, z_lo: 4; z = z_hi * 4 + z_lo), core: 2. Of those that a mesh axis runs over, the one named last changes fastest.
Arguments:
- queries: bfloat16 [4, 64, 384, 768], P('dp', 'sp'), may hold values from -7 to 7
- keys: bfloat16 [4, 64, 384, 768], P('dp', 'sp'), may hold values from -7 to 7
- values: bfloat16 [4, 64, 384, 768], P('dp', 'sp'), may hold values from -6 to 6
- tile_lists: int32 [64, 5], P('sp'), may hold values from -1 to 63, as said below
- grad_out: bfloat16 [4, 64, 384, 3072], P('dp', 'sp'), may hold values from -16 to 16
- w_out: bfloat16 [768, 3072], replicated, may hold values from -0.21875 to 0.21875
Outputs:
- grad_queries: bfloat16 [4, 64, 384, 768], P('dp', 'sp')
- grad_keys: bfloat16 [4, 64, 384, 768], P('dp', 'sp')
- grad_values: bfloat16 [4, 64, 384, 768], P('dp', 'sp')
- grad_w_out: float32 [768, 3072], P('dp', 'sp')
The draws below stay inside these ranges and needn't reach their ends.
Inputs may be any that keep to these rules, and one draw needn't show every extreme that they name: `tile_lists`: row i lists distinct tiles of the 3 x 3 block of time-height tile positions around tile i (clipped at the clip's borders), tile i itself first; -1 marks an empty entry and comes only after all tiles of the clipped block are listed.
All inputs are finite; a program needn't handle non-finite values.
Results may differ from the reference program's by a relative error of at most 0.014.
The reference program's roundings to bfloat16 on the way count: a program that leaves them out, or rounds other values in their place, can miss the bound.
Values may be sent and summed in bfloat16 or wider, within the bound.
No kernel may reach another device: no remote copies, remote signals or barrier semaphores. Data moves between devices by JAX's collectives and lax.ppermute only.
A program may use at most 128 MiB of HBM per device.

```python
import math
import jax
import jax.numpy as jnp
from jax import lax

D = 3072
HEADS = 6
HEAD = 128
TILE_TOK = 384
NB = 5
H_TILES = 4
INNER = 768
TILES = 64
T_TILES = 16
CLIPS = 4


def query_key_pair(key):
    base_key = jax.random.fold_in(key, 7)
    query_seed, key_seed = jax.random.split(base_key, 2)
    shape_all = (CLIPS, TILES, TILE_TOK, INNER)
    query_draw = jnp.clip(jax.random.normal(query_seed, shape_all, jnp.float32), -6.0, 6.0)
    key_draw = jnp.clip(jax.random.normal(key_seed, shape_all, jnp.float32), -6.0, 6.0)
    return (query_draw, key_draw)


def draw_queries(key, part):
    return query_key_pair(key)[0].astype(jnp.bfloat16)


def draw_keys(key, part):
    return query_key_pair(key)[1].astype(jnp.bfloat16)


def draw_tile_lists(key, part):
    tile_ids = jnp.arange(TILES, dtype=jnp.int32)
    time_row = tile_ids // H_TILES
    height_col = tile_ids % H_TILES
    slot_ids = jnp.arange(9, dtype=jnp.int32)
    time_step = slot_ids // 3 - 1
    height_step = slot_ids % 3 - 1
    near_time = time_row[:, None] + time_step[None, :]
    near_height = height_col[:, None] + height_step[None, :]
    inside = (near_time >= 0) & (near_time < T_TILES) & (near_height >= 0) & (near_height < H_TILES)
    near_ids = near_time * H_TILES + near_height
    noise = jax.random.randint(jax.random.fold_in(key, 3), (TILES, 9), 0, 1000, dtype=jnp.int32)
    ranking = noise * 16 + slot_ids[None, :] + jnp.where(inside, 100000, 0) + jnp.where(slot_ids[None, :] == 4, 1000000, 0)
    top_scores, order = lax.top_k(ranking, NB)
    chosen_inside = jnp.take_along_axis(inside, order, axis=1)
    chosen_ids = jnp.take_along_axis(near_ids, order, axis=1)
    return jnp.where(chosen_inside, chosen_ids, -1).astype(jnp.int32)


def raised(drawn, key, source, target, shards_of, factor):
    owner, partner = [(jnp.arange(drawn.shape[dim]) // (drawn.shape[dim] // shards_of)).reshape([-1 if axis == dim else 1 for axis in range(drawn.ndim)]) for dim in (source, target)]
    chosen = jax.random.permutation(key, shards_of)[partner]
    strong = (owner == chosen) | (owner == (partner + shards_of // 2) % shards_of)
    return jnp.where(strong, factor * drawn, drawn)


def shard_levels(own_key, shape, shards, low, high):
    level, own = 1.0, jax.random.fold_in(own_key, 6)
    for axis_at, parts in shards:
        steps = jnp.exp(jax.random.uniform(jax.random.fold_in(own, axis_at), (parts,), jnp.float32, low / len(shards), high / len(shards)))
        level = level * jnp.repeat(steps, shape[axis_at] // parts).reshape([-1 if axis == axis_at else 1 for axis in range(len(shape))])
    return level


def scatter_about(key, extent, spread, most, cuts=(), kind=jnp.bfloat16):
    drawn = spread * jax.random.normal(key, extent, jnp.float32)
    if cuts:
        drawn = drawn * shard_levels(key, extent, cuts, -0.22, 0.18)
    return jnp.clip(drawn, -most, most).astype(kind)


def bell_draw_with(stream_key, extent, width, most, pieces, heavy, kind=jnp.bfloat16):
    entries = width * jax.random.normal(stream_key, extent, jnp.float32)
    if pieces:
        entries = entries * shard_levels(stream_key, extent, pieces, -0.22, 0.18)
    return jnp.clip(raised(entries, jax.random.fold_in(stream_key, 3), *heavy), -most, most).astype(kind)


def setup_inputs(seed: int = 0) -> dict:
    key_list = jax.random.split(jax.random.key(seed), 7)
    queries = draw_queries(jax.random.fold_in(key_list[6], 71), 0)
    keys = draw_keys(jax.random.fold_in(key_list[6], 71), 0)
    values = scatter_about(key_list[2], (CLIPS, TILES, TILE_TOK, INNER), 1.0, 6.0, ((0, 4), (1, 64)))
    tile_lists = draw_tile_lists(jax.random.fold_in(key_list[6], 71), 0)
    grad_out = bell_draw_with(key_list[4], (CLIPS, TILES, TILE_TOK, D), 1.0, 16.0, ((0, 4), (1, 64)), (1, 3, 64, 4.0))
    w_out = scatter_about(key_list[5], (INNER, D), INNER ** -0.5, 0.21875)
    return {"queries": queries, "keys": keys, "values": values, "tile_lists": tile_lists, "grad_out": grad_out, "w_out": w_out}


def reference(queries, keys, values, tile_lists, grad_out, w_out):
    score_scale = 1.0 / math.sqrt(HEAD)

    def one_clip(clip_args):
        query_all, key_all, value_all, grad_all = clip_args
        grad_attn = jnp.dot(grad_all.reshape(TILES * TILE_TOK, D), w_out.T, preferred_element_type=jnp.float32)
        grad_attn = grad_attn.astype(jnp.bfloat16).reshape(TILES, TILE_TOK, INNER)
        empty_acc = jnp.zeros((TILES, TILE_TOK, INNER), jnp.float32)

        def tile_step(carry, tile_index):
            key_acc, value_acc = carry
            listed = tile_lists[tile_index]
            valid_slot = listed >= 0
            safe_ids = jnp.where(valid_slot, listed, tile_index).astype(jnp.int32)
            key_rows = key_all[safe_ids].astype(jnp.float32).reshape(NB * TILE_TOK, HEADS, HEAD)
            value_rows = value_all[safe_ids].astype(jnp.float32).reshape(NB * TILE_TOK, HEADS, HEAD)
            query_tile = query_all[tile_index].astype(jnp.float32).reshape(TILE_TOK, HEADS, HEAD)
            grad_tile = grad_attn[tile_index].astype(jnp.float32).reshape(TILE_TOK, HEADS, HEAD)
            key_mask = jnp.repeat(valid_slot, TILE_TOK)
            scores = jnp.einsum('qhd,khd->hqk', query_tile, key_rows) * score_scale
            scores = jnp.where(key_mask[None, None, :], scores, -1e+30)
            row_peak = lax.optimization_barrier(jnp.max(scores, axis=2, keepdims=True))
            exp_scores = jnp.exp(scores - row_peak)
            attn_probs = exp_scores / lax.optimization_barrier(jnp.sum(exp_scores, axis=2, keepdims=True))
            probs_low = lax.optimization_barrier(attn_probs.astype(jnp.bfloat16)).astype(jnp.float32)
            attn_tile = jnp.einsum('hqk,khd->qhd', probs_low, value_rows).astype(jnp.bfloat16)
            attn_wide = lax.optimization_barrier(attn_tile).astype(jnp.float32)
            row_delta = jnp.einsum('qhd,qhd->hq', grad_tile, attn_wide)
            dprobs = jnp.einsum('qhd,khd->hqk', grad_tile, value_rows)
            dscores = (attn_probs * (dprobs - row_delta[:, :, None])).astype(jnp.bfloat16)
            dscores = lax.optimization_barrier(dscores).astype(jnp.float32)
            grad_query = (jnp.einsum('hqk,khd->qhd', dscores, key_rows) * score_scale).astype(jnp.bfloat16)
            key_part = (jnp.einsum('hqk,qhd->khd', dscores, query_tile) * score_scale).astype(jnp.bfloat16)
            value_part = jnp.einsum('hqk,qhd->khd', probs_low, grad_tile).astype(jnp.bfloat16)
            key_part = lax.optimization_barrier(key_part).astype(jnp.float32).reshape(NB, TILE_TOK, INNER)
            value_part = lax.optimization_barrier(value_part).astype(jnp.float32).reshape(NB, TILE_TOK, INNER)
            keep_mask = valid_slot[:, None, None]
            key_acc = key_acc.at[safe_ids].add(jnp.where(keep_mask, key_part, jnp.float32(0.0)))
            value_acc = value_acc.at[safe_ids].add(jnp.where(keep_mask, value_part, jnp.float32(0.0)))
            return ((key_acc, value_acc), (grad_query.reshape(TILE_TOK, INNER), attn_tile.reshape(TILE_TOK, INNER)))
        (key_acc, value_acc), (grad_query, attn_all) = lax.scan(tile_step, (empty_acc, empty_acc), jnp.arange(TILES, dtype=jnp.int32))
        weight_term = jnp.dot(attn_all.reshape(TILES * TILE_TOK, INNER).T, grad_all.reshape(TILES * TILE_TOK, D), preferred_element_type=jnp.float32)
        return (grad_query, key_acc.astype(jnp.bfloat16), value_acc.astype(jnp.bfloat16), weight_term)
    results = lax.map(one_clip, (queries, keys, values, grad_out))
    return (results[0], results[1], results[2], lax.optimization_barrier(jnp.sum(results[3], axis=0)))
```

```python
import math

import jax
import jax.numpy as jnp
from jax import lax
from jax.sharding import PartitionSpec as P

HEAD = 128
H_TILES = 4


def from_behind(value, axis, steps):
    count = lax.axis_size(axis)
    initial, last = (max(0, -steps), min(count, count - steps))
    return lax.ppermute(value, axis, [(source, source + steps) for source in range(initial, last)])


def body(queries, keys, values, tile_lists, grad_out, w_out):
    query_tile = queries[0, 0]
    key_tile = keys[0, 0]
    value_tile = values[0, 0]
    grad_tile = grad_out[0, 0]
    listed = tile_lists[0]
    tile_tok, inner_width = query_tile.shape
    slot_count = listed.shape[0]
    height_tiles = H_TILES
    score_scale = 1.0 / math.sqrt(HEAD)
    own_tile = lax.axis_index("sp")
    key_value = jnp.stack([key_tile, value_tile])
    offsets = [(time_step, height_step) for time_step in (-1, 0, 1) for height_step in (-1, 0, 1)]
    pieces = []
    for time_step, height_step in offsets:
        if time_step == 0 and height_step == 0:
            pieces.append(key_value)
        else:
            pieces.append(from_behind(key_value, "sp", -(time_step * height_tiles + height_step)))
    window = jnp.stack(pieces)
    valid_slot = listed >= 0
    time_gap = listed // height_tiles - own_tile // height_tiles
    height_gap = listed % height_tiles - own_tile % height_tiles
    slot_index = jnp.where(valid_slot, (time_gap + 1) * 3 + height_gap + 1, 4)
    picked = jnp.take(window, slot_index, axis=0)
    key_rows = picked[:, 0].reshape(slot_count * tile_tok, inner_width)
    value_rows = picked[:, 1].reshape(slot_count * tile_tok, inner_width)
    key_mask = jnp.repeat(valid_slot, tile_tok)
    grad_attn = lax.dot_general(
        grad_tile, w_out, (((1,), (1,)), ((), ())), preferred_element_type=jnp.float32
    ).astype(jnp.bfloat16)
    block_width = 128
    heads_block = block_width // HEAD

    def head_block(block_index, carry):
        attn_all, grad_query, grad_key, grad_value = carry
        block_start = block_index * block_width
        query_part = lax.dynamic_slice_in_dim(query_tile, block_start, block_width, 1).reshape(
            tile_tok, heads_block, HEAD
        )
        key_part = lax.dynamic_slice_in_dim(key_rows, block_start, block_width, 1).reshape(
            -1, heads_block, HEAD
        )
        value_part = lax.dynamic_slice_in_dim(value_rows, block_start, block_width, 1).reshape(
            -1, heads_block, HEAD
        )
        grad_part = lax.dynamic_slice_in_dim(grad_attn, block_start, block_width, 1).reshape(
            tile_tok, heads_block, HEAD
        )
        scores = (
            jnp.einsum("qhd,khd->hqk", query_part, key_part, preferred_element_type=jnp.float32)
            * score_scale
        )
        scores = jnp.where(key_mask[None, None, :], scores, -1e30)
        row_peak = jnp.max(scores, axis=2, keepdims=True)
        exp_scores = jnp.exp(scores - row_peak)
        attn_probs = exp_scores / jnp.sum(exp_scores, axis=2, keepdims=True)
        probs_low = attn_probs.astype(jnp.bfloat16)
        attn_part = jnp.einsum(
            "hqk,khd->qhd", probs_low, value_part, preferred_element_type=jnp.float32
        ).astype(jnp.bfloat16)
        row_delta = jnp.einsum(
            "qhd,qhd->hq", grad_part.astype(jnp.float32), attn_part.astype(jnp.float32)
        )
        dprobs = jnp.einsum(
            "qhd,khd->hqk", grad_part, value_part, preferred_element_type=jnp.float32
        )
        dscores = (attn_probs * (dprobs - row_delta[:, :, None])).astype(jnp.bfloat16)
        query_grad = (
            jnp.einsum("hqk,khd->qhd", dscores, key_part, preferred_element_type=jnp.float32)
            * score_scale
        )
        key_grad = (
            jnp.einsum("hqk,qhd->khd", dscores, query_part, preferred_element_type=jnp.float32)
            * score_scale
        )
        value_grad = jnp.einsum(
            "hqk,qhd->khd", probs_low, grad_part, preferred_element_type=jnp.float32
        )
        attn_all = lax.dynamic_update_slice_in_dim(
            attn_all, attn_part.reshape(tile_tok, block_width), block_start, 1
        )
        grad_query = lax.dynamic_update_slice_in_dim(
            grad_query,
            query_grad.astype(jnp.bfloat16).reshape(tile_tok, block_width),
            block_start,
            1,
        )
        grad_key = lax.dynamic_update_slice_in_dim(
            grad_key, key_grad.astype(jnp.bfloat16).reshape(-1, block_width), block_start, 1
        )
        grad_value = lax.dynamic_update_slice_in_dim(
            grad_value, value_grad.astype(jnp.bfloat16).reshape(-1, block_width), block_start, 1
        )
        return (attn_all, grad_query, grad_key, grad_value)

    start_state = (
        jnp.zeros((tile_tok, inner_width), jnp.bfloat16),
        jnp.zeros((tile_tok, inner_width), jnp.bfloat16),
        jnp.zeros((slot_count * tile_tok, inner_width), jnp.bfloat16),
        jnp.zeros((slot_count * tile_tok, inner_width), jnp.bfloat16),
    )
    attn_all, grad_query, grad_key, grad_value = lax.fori_loop(
        0, inner_width // block_width, head_block, start_state
    )
    dp_count = lax.axis_size("dp")
    sp_count = lax.axis_size("sp")
    dp_index = lax.axis_index("dp")
    core, high = dp_index % 2, dp_index // 2
    row_block = inner_width // dp_count
    model_width = grad_tile.shape[1]
    col_block = model_width // sp_count
    attn_blocks = attn_all.reshape(tile_tok, dp_count // 2, 2, row_block)
    kept_rows = lax.dynamic_index_in_dim(attn_blocks, core, 2, keepdims=False).reshape(tile_tok, -1)
    sent_rows = lax.dynamic_index_in_dim(attn_blocks, 1 - core, 2, keepdims=False).reshape(tile_tok, -1)
    contract_tokens = (((0,), (0,)), ((), ()))
    kept_part = lax.dot_general(grad_tile, kept_rows, contract_tokens, preferred_element_type=jnp.float32)
    sent_part = lax.dot_general(grad_tile, sent_rows, contract_tokens, preferred_element_type=jnp.float32)
    sibling_part = lax.ppermute(
        sent_part.astype(jnp.bfloat16), "dp", [(index, index ^ 1) for index in range(dp_count)]
    )
    core_sum = (kept_part + sibling_part.astype(jnp.float32)).astype(jnp.bfloat16)
    by_column = lax.all_to_all(
        core_sum.reshape(sp_count, col_block, -1), "sp", 0, 0, tiled=True
    )
    column_sum = by_column.astype(jnp.float32).sum(0).reshape(col_block, dp_count // 2, row_block)
    own_half = lax.dynamic_index_in_dim(column_sum, high, 1, keepdims=False)
    other_half = lax.dynamic_index_in_dim(column_sum, 1 - high, 1, keepdims=False)
    weight_grad = (
        own_half
        + lax.ppermute(other_half, "dp", [(index, (index + 2) % dp_count) for index in range(dp_count)])
    ).T
    slot_terms = jnp.stack(
        [
            grad_key.reshape(slot_count, tile_tok, inner_width),
            grad_value.reshape(slot_count, tile_tok, inner_width),
        ],
        axis=1,
    )
    selector = (
        (slot_index[:, None] == jnp.arange(9, dtype=jnp.int32)[None, :]) & valid_slot[:, None]
    ).astype(jnp.bfloat16)
    by_slot = jnp.einsum(
        "js,jctd->sctd", selector, slot_terms, preferred_element_type=jnp.float32
    ).astype(jnp.bfloat16)
    grad_total = by_slot[4].astype(jnp.float32)
    for time_step, height_step in offsets:
        if time_step == 0 and height_step == 0:
            continue
        slot_number = (time_step + 1) * 3 + height_step + 1
        arrived = from_behind(by_slot[slot_number], "sp", time_step * height_tiles + height_step)
        grad_total = grad_total + arrived.astype(jnp.float32)
    grad_kv = grad_total.astype(jnp.bfloat16)
    return (grad_query[None, None], grad_kv[0][None, None], grad_kv[1][None, None], weight_grad)


def solution(mesh):
    in_specs = (
        P("dp", "sp", None, None),
        P("dp", "sp", None, None),
        P("dp", "sp", None, None),
        P("sp", None),
        P("dp", "sp", None, None),
        P(),
    )
    out_specs = (
        P("dp", "sp", None, None),
        P("dp", "sp", None, None),
        P("dp", "sp", None, None),
        P("dp", "sp"),
    )
    return jax.shard_map(body, mesh=mesh, in_specs=in_specs, out_specs=out_specs, check_vma=False)
```

```python
import math

import jax
import jax.numpy as jnp
from jax import lax
from jax.sharding import PartitionSpec as P

HEAD = 128
H_TILES = 4


def neighbour_shift(value, axis, time_step, height_step, height_tiles, toward):
    count = lax.axis_size(axis)
    time_tiles = count // height_tiles
    offset = time_step * height_tiles + height_step
    pairs = []
    for tile in range(count):
        time_row, height_col = divmod(tile, height_tiles)
        if 0 <= time_row + time_step < time_tiles and 0 <= height_col + height_step < height_tiles:
            pairs.append((tile, tile + offset) if toward else (tile + offset, tile))
    return lax.ppermute(value, axis, pairs)


def body(queries, keys, values, tile_lists, grad_out, w_out):
    query_tile = queries[0, 0]
    key_tile = keys[0, 0]
    value_tile = values[0, 0]
    grad_tile = grad_out[0, 0]
    listed = tile_lists[0]
    tile_tok, inner_width = query_tile.shape
    slot_count = listed.shape[0]
    height_tiles = H_TILES
    score_scale = 1.0 / math.sqrt(HEAD)
    own_tile = lax.axis_index("sp")
    key_value = jnp.stack([key_tile, value_tile])
    offsets = [(time_step, height_step) for time_step in (-1, 0, 1) for height_step in (-1, 0, 1)]
    pieces = []
    for time_step, height_step in offsets:
        if time_step == 0 and height_step == 0:
            pieces.append(key_value)
        else:
            pieces.append(neighbour_shift(key_value, "sp", time_step, height_step, height_tiles, False))
    window = jnp.stack(pieces)
    valid_slot = listed >= 0
    time_gap = listed // height_tiles - own_tile // height_tiles
    height_gap = listed % height_tiles - own_tile % height_tiles
    slot_index = jnp.where(valid_slot, (time_gap + 1) * 3 + height_gap + 1, 4)
    picked = jnp.take(window, slot_index, axis=0)
    key_rows = picked[:, 0].reshape(slot_count * tile_tok, inner_width)
    value_rows = picked[:, 1].reshape(slot_count * tile_tok, inner_width)
    key_mask = jnp.repeat(valid_slot, tile_tok)
    grad_attn = lax.dot_general(
        grad_tile, w_out, (((1,), (1,)), ((), ())), preferred_element_type=jnp.float32
    ).astype(jnp.bfloat16)
    block_width = 128
    heads_block = block_width // HEAD

    def head_block(block_index, carry):
        attn_all, grad_query, grad_key, grad_value = carry
        block_start = block_index * block_width
        query_part = lax.dynamic_slice_in_dim(query_tile, block_start, block_width, 1).reshape(
            tile_tok, heads_block, HEAD
        )
        key_part = lax.dynamic_slice_in_dim(key_rows, block_start, block_width, 1).reshape(
            -1, heads_block, HEAD
        )
        value_part = lax.dynamic_slice_in_dim(value_rows, block_start, block_width, 1).reshape(
            -1, heads_block, HEAD
        )
        grad_part = lax.dynamic_slice_in_dim(grad_attn, block_start, block_width, 1).reshape(
            tile_tok, heads_block, HEAD
        )
        scores = (
            jnp.einsum("qhd,khd->hqk", query_part, key_part, preferred_element_type=jnp.float32)
            * score_scale
        )
        scores = jnp.where(key_mask[None, None, :], scores, -1e30)
        row_peak = jnp.max(scores, axis=2, keepdims=True)
        exp_scores = jnp.exp(scores - row_peak)
        attn_probs = exp_scores / jnp.sum(exp_scores, axis=2, keepdims=True)
        probs_low = attn_probs.astype(jnp.bfloat16)
        attn_part = jnp.einsum(
            "hqk,khd->qhd", probs_low, value_part, preferred_element_type=jnp.float32
        ).astype(jnp.bfloat16)
        row_delta = jnp.einsum(
            "qhd,qhd->hq", grad_part.astype(jnp.float32), attn_part.astype(jnp.float32)
        )
        dprobs = jnp.einsum(
            "qhd,khd->hqk", grad_part, value_part, preferred_element_type=jnp.float32
        )
        dscores = (attn_probs * (dprobs - row_delta[:, :, None])).astype(jnp.bfloat16)
        query_grad = (
            jnp.einsum("hqk,khd->qhd", dscores, key_part, preferred_element_type=jnp.float32)
            * score_scale
        )
        key_grad = (
            jnp.einsum("hqk,qhd->khd", dscores, query_part, preferred_element_type=jnp.float32)
            * score_scale
        )
        value_grad = jnp.einsum(
            "hqk,qhd->khd", probs_low, grad_part, preferred_element_type=jnp.float32
        )
        attn_all = lax.dynamic_update_slice_in_dim(
            attn_all, attn_part.reshape(tile_tok, block_width), block_start, 1
        )
        grad_query = lax.dynamic_update_slice_in_dim(
            grad_query,
            query_grad.astype(jnp.bfloat16).reshape(tile_tok, block_width),
            block_start,
            1,
        )
        grad_key = lax.dynamic_update_slice_in_dim(
            grad_key, key_grad.astype(jnp.bfloat16).reshape(-1, block_width), block_start, 1
        )
        grad_value = lax.dynamic_update_slice_in_dim(
            grad_value, value_grad.astype(jnp.bfloat16).reshape(-1, block_width), block_start, 1
        )
        return (attn_all, grad_query, grad_key, grad_value)

    start_state = (
        jnp.zeros((tile_tok, inner_width), jnp.bfloat16),
        jnp.zeros((tile_tok, inner_width), jnp.bfloat16),
        jnp.zeros((slot_count * tile_tok, inner_width), jnp.bfloat16),
        jnp.zeros((slot_count * tile_tok, inner_width), jnp.bfloat16),
    )
    attn_all, grad_query, grad_key, grad_value = lax.fori_loop(
        0, inner_width // block_width, head_block, start_state
    )
    dp_count = lax.axis_size("dp")
    sp_count = lax.axis_size("sp")
    dp_index = lax.axis_index("dp")
    core, high = dp_index % 2, dp_index // 2
    row_block = inner_width // dp_count
    model_width = grad_tile.shape[1]
    col_block = model_width // sp_count
    attn_blocks = attn_all.reshape(tile_tok, dp_count // 2, 2, row_block)
    kept_rows = lax.dynamic_index_in_dim(attn_blocks, core, 2, keepdims=False).reshape(tile_tok, -1)
    sent_rows = lax.dynamic_index_in_dim(attn_blocks, 1 - core, 2, keepdims=False).reshape(tile_tok, -1)
    contract_tokens = (((0,), (0,)), ((), ()))
    kept_part = lax.dot_general(grad_tile, kept_rows, contract_tokens, preferred_element_type=jnp.float32)
    sent_part = lax.dot_general(grad_tile, sent_rows, contract_tokens, preferred_element_type=jnp.float32)
    sibling_part = lax.ppermute(
        sent_part.astype(jnp.bfloat16), "dp", [(index, index ^ 1) for index in range(dp_count)]
    )
    core_sum = (kept_part + sibling_part.astype(jnp.float32)).astype(jnp.bfloat16)
    by_column = lax.all_to_all(
        core_sum.reshape(sp_count, col_block, -1), "sp", 0, 0, tiled=True
    )
    column_sum = by_column.astype(jnp.float32).sum(0).reshape(col_block, dp_count // 2, row_block)
    own_half = lax.dynamic_index_in_dim(column_sum, high, 1, keepdims=False)
    other_half = lax.dynamic_index_in_dim(column_sum, 1 - high, 1, keepdims=False)
    weight_grad = (
        own_half
        + lax.ppermute(other_half, "dp", [(index, (index + 2) % dp_count) for index in range(dp_count)])
    ).T
    key_terms = grad_key.reshape(slot_count, tile_tok, inner_width)
    value_terms = grad_value.reshape(slot_count, tile_tok, inner_width)
    matches = (slot_index[:, None] == jnp.arange(9, dtype=jnp.int32)[None, :]) & valid_slot[:, None]
    match_slot = jnp.argmax(matches, axis=0)
    match_any = jnp.any(matches, axis=0)

    def slot_payload(slot_number):
        picked_slot = match_slot[slot_number]
        payload = jnp.stack(
            [
                lax.dynamic_index_in_dim(key_terms, picked_slot, 0, keepdims=False),
                lax.dynamic_index_in_dim(value_terms, picked_slot, 0, keepdims=False),
            ]
        )
        return jnp.where(match_any[slot_number], payload, jnp.zeros_like(payload))

    grad_total = slot_payload(4).astype(jnp.float32)
    for time_step, height_step in offsets:
        if time_step == 0 and height_step == 0:
            continue
        slot_number = (time_step + 1) * 3 + height_step + 1
        arrived = neighbour_shift(
            slot_payload(slot_number), "sp", time_step, height_step, height_tiles, True
        )
        grad_total = grad_total + arrived.astype(jnp.float32)
    grad_kv = grad_total.astype(jnp.bfloat16)
    return (grad_query[None, None], grad_kv[0][None, None], grad_kv[1][None, None], weight_grad)


def solution(mesh):
    in_specs = (
        P("dp", "sp", None, None),
        P("dp", "sp", None, None),
        P("dp", "sp", None, None),
        P("sp", None),
        P("dp", "sp", None, None),
        P(),
    )
    out_specs = (
        P("dp", "sp", None, None),
        P("dp", "sp", None, None),
        P("dp", "sp", None, None),
        P("dp", "sp"),
    )
    return jax.shard_map(body, mesh=mesh, in_specs=in_specs, out_specs=out_specs, check_vma=False)
```

```python
import functools
import math

import jax
import jax.numpy as jnp
from jax import lax
from jax.experimental import pallas as pl
from jax.sharding import PartitionSpec as P

HEAD = 128
H_TILES = 4


def neighbour_shift(value, axis, time_step, height_step, height_tiles, toward):
    count = lax.axis_size(axis)
    time_tiles = count // height_tiles
    offset = time_step * height_tiles + height_step
    pairs = []
    for tile in range(count):
        time_row, height_col = divmod(tile, height_tiles)
        if 0 <= time_row + time_step < time_tiles and 0 <= height_col + height_step < height_tiles:
            pairs.append((tile, tile + offset) if toward else (tile + offset, tile))
    return lax.ppermute(value, axis, pairs)


def tile_attention(mask_ref, query_ref, key_ref, value_ref, grad_ref, attn_ref, dq_ref, dk_ref, dv_ref, *, score_scale):
    rows_by_rows = (((1,), (1,)), ((), ()))
    cols_by_cols = (((0,), (0,)), ((), ()))
    query = query_ref[...]
    key = key_ref[...]
    value = value_ref[...]
    grad = grad_ref[...]
    scores = lax.dot_general(query, key, rows_by_rows, preferred_element_type=jnp.float32) * score_scale
    scores = jnp.where(mask_ref[...] > 0, scores, -1e30)
    row_peak = jnp.max(scores, axis=1, keepdims=True)
    exp_scores = jnp.exp(scores - row_peak)
    probs = exp_scores / jnp.sum(exp_scores, axis=1, keepdims=True)
    probs_low = probs.astype(jnp.bfloat16)
    attn = jnp.dot(probs_low, value, preferred_element_type=jnp.float32).astype(jnp.bfloat16)
    attn_ref[...] = attn
    row_delta = jnp.sum(grad.astype(jnp.float32) * attn.astype(jnp.float32), axis=1, keepdims=True)
    dprobs = lax.dot_general(grad, value, rows_by_rows, preferred_element_type=jnp.float32)
    dscores = (probs * (dprobs - row_delta)).astype(jnp.bfloat16)
    dq_ref[...] = (jnp.dot(dscores, key, preferred_element_type=jnp.float32) * score_scale).astype(jnp.bfloat16)
    dk_ref[...] = (
        lax.dot_general(dscores, query, cols_by_cols, preferred_element_type=jnp.float32) * score_scale
    ).astype(jnp.bfloat16)
    dv_ref[...] = lax.dot_general(probs_low, grad, cols_by_cols, preferred_element_type=jnp.float32).astype(jnp.bfloat16)


def body(queries, keys, values, tile_lists, grad_out, w_out):
    query_tile = queries[0, 0]
    key_tile = keys[0, 0]
    value_tile = values[0, 0]
    grad_tile = grad_out[0, 0]
    listed = tile_lists[0]
    tile_tok, inner_width = query_tile.shape
    slot_count = listed.shape[0]
    height_tiles = H_TILES
    score_scale = 1.0 / math.sqrt(HEAD)
    own_tile = lax.axis_index("sp")
    key_value = jnp.stack([key_tile, value_tile])
    offsets = [(time_step, height_step) for time_step in (-1, 0, 1) for height_step in (-1, 0, 1)]
    pieces = []
    for time_step, height_step in offsets:
        if time_step == 0 and height_step == 0:
            pieces.append(key_value)
        else:
            pieces.append(neighbour_shift(key_value, "sp", time_step, height_step, height_tiles, False))
    window = jnp.stack(pieces)
    valid_slot = listed >= 0
    time_gap = listed // height_tiles - own_tile // height_tiles
    height_gap = listed % height_tiles - own_tile % height_tiles
    slot_index = jnp.where(valid_slot, (time_gap + 1) * 3 + height_gap + 1, 4)
    picked = jnp.take(window, slot_index, axis=0)
    key_rows = picked[:, 0].reshape(slot_count * tile_tok, inner_width)
    value_rows = picked[:, 1].reshape(slot_count * tile_tok, inner_width)
    key_mask = jnp.repeat(valid_slot, tile_tok)
    grad_attn = lax.dot_general(
        grad_tile, w_out, (((1,), (1,)), ((), ())), preferred_element_type=jnp.float32
    ).astype(jnp.bfloat16)
    key_count = slot_count * tile_tok
    mask_row = key_mask.astype(jnp.int32).reshape(1, key_count)
    head_count = inner_width // HEAD
    tile_spec = pl.BlockSpec((tile_tok, HEAD), lambda head: (0, head))
    key_spec = pl.BlockSpec((key_count, HEAD), lambda head: (0, head))
    attn_all, grad_query, grad_key, grad_value = pl.pallas_call(
        functools.partial(tile_attention, score_scale=score_scale),
        grid=(head_count,),
        in_specs=[
            pl.BlockSpec((1, key_count), lambda head: (0, 0)),
            tile_spec,
            key_spec,
            key_spec,
            tile_spec,
        ],
        out_specs=[tile_spec, tile_spec, key_spec, key_spec],
        out_shape=[
            jax.ShapeDtypeStruct((tile_tok, inner_width), jnp.bfloat16),
            jax.ShapeDtypeStruct((tile_tok, inner_width), jnp.bfloat16),
            jax.ShapeDtypeStruct((key_count, inner_width), jnp.bfloat16),
            jax.ShapeDtypeStruct((key_count, inner_width), jnp.bfloat16),
        ],
        cost_estimate=pl.CostEstimate(
            flops=2 * 5 * tile_tok * key_count * inner_width,
            transcendentals=head_count * tile_tok * key_count,
            bytes_accessed=2 * 2 * (2 * tile_tok + 2 * key_count) * inner_width,
        ),
    )(mask_row, query_tile, key_rows, value_rows, grad_attn)
    dp_count = lax.axis_size("dp")
    sp_count = lax.axis_size("sp")
    dp_index = lax.axis_index("dp")
    core, high = dp_index % 2, dp_index // 2
    row_block = inner_width // dp_count
    model_width = grad_tile.shape[1]
    col_block = model_width // sp_count
    attn_blocks = attn_all.reshape(tile_tok, dp_count // 2, 2, row_block)
    kept_rows = lax.dynamic_index_in_dim(attn_blocks, core, 2, keepdims=False).reshape(tile_tok, -1)
    sent_rows = lax.dynamic_index_in_dim(attn_blocks, 1 - core, 2, keepdims=False).reshape(tile_tok, -1)
    contract_tokens = (((0,), (0,)), ((), ()))
    kept_part = lax.dot_general(grad_tile, kept_rows, contract_tokens, preferred_element_type=jnp.float32)
    sent_part = lax.dot_general(grad_tile, sent_rows, contract_tokens, preferred_element_type=jnp.float32)
    sibling_part = lax.ppermute(
        sent_part.astype(jnp.bfloat16), "dp", [(index, index ^ 1) for index in range(dp_count)]
    )
    core_sum = (kept_part + sibling_part.astype(jnp.float32)).astype(jnp.bfloat16)
    by_column = lax.all_to_all(
        core_sum.reshape(sp_count, col_block, -1), "sp", 0, 0, tiled=True
    )
    column_sum = by_column.astype(jnp.float32).sum(0).reshape(col_block, dp_count // 2, row_block)
    own_half = lax.dynamic_index_in_dim(column_sum, high, 1, keepdims=False)
    other_half = lax.dynamic_index_in_dim(column_sum, 1 - high, 1, keepdims=False)
    weight_grad = (
        own_half
        + lax.ppermute(other_half, "dp", [(index, (index + 2) % dp_count) for index in range(dp_count)])
    ).T
    key_terms = grad_key.reshape(slot_count, tile_tok, inner_width)
    value_terms = grad_value.reshape(slot_count, tile_tok, inner_width)
    matches = (slot_index[:, None] == jnp.arange(9, dtype=jnp.int32)[None, :]) & valid_slot[:, None]
    match_slot = jnp.argmax(matches, axis=0)
    match_any = jnp.any(matches, axis=0)

    def slot_payload(slot_number):
        picked_slot = match_slot[slot_number]
        payload = jnp.stack(
            [
                lax.dynamic_index_in_dim(key_terms, picked_slot, 0, keepdims=False),
                lax.dynamic_index_in_dim(value_terms, picked_slot, 0, keepdims=False),
            ]
        )
        return jnp.where(match_any[slot_number], payload, jnp.zeros_like(payload))

    grad_total = slot_payload(4).astype(jnp.float32)
    for time_step, height_step in offsets:
        if time_step == 0 and height_step == 0:
            continue
        slot_number = (time_step + 1) * 3 + height_step + 1
        arrived = neighbour_shift(
            slot_payload(slot_number), "sp", time_step, height_step, height_tiles, True
        )
        grad_total = grad_total + arrived.astype(jnp.float32)
    grad_kv = grad_total.astype(jnp.bfloat16)
    return (grad_query[None, None], grad_kv[0][None, None], grad_kv[1][None, None], weight_grad)


def solution(mesh):
    in_specs = (
        P("dp", "sp", None, None),
        P("dp", "sp", None, None),
        P("dp", "sp", None, None),
        P("sp", None),
        P("dp", "sp", None, None),
        P(),
    )
    out_specs = (
        P("dp", "sp", None, None),
        P("dp", "sp", None, None),
        P("dp", "sp", None, None),
        P("dp", "sp"),
    )
    return jax.shard_map(body, mesh=mesh, in_specs=in_specs, out_specs=out_specs, check_vma=False)
```

```python
import functools
import math

import jax
import jax.numpy as jnp
from jax import lax
from jax.experimental import pallas as pl
from jax.sharding import PartitionSpec as P

HEAD = 128
H_TILES = 4


def neighbour_shift(value, axis, time_step, height_step, height_tiles, toward):
    count = lax.axis_size(axis)
    time_tiles = count // height_tiles
    offset = time_step * height_tiles + height_step
    pairs = []
    for tile in range(count):
        time_row, height_col = divmod(tile, height_tiles)
        if 0 <= time_row + time_step < time_tiles and 0 <= height_col + height_step < height_tiles:
            pairs.append((tile, tile + offset) if toward else (tile + offset, tile))
    return lax.ppermute(value, axis, pairs)


def tile_attention(mask_ref, query_ref, key_ref, value_ref, grad_ref, attn_ref, dq_ref, dk_ref, dv_ref, *, score_scale):
    rows_by_rows = (((1,), (1,)), ((), ()))
    cols_by_cols = (((0,), (0,)), ((), ()))
    query = query_ref[...]
    key = key_ref[...]
    value = value_ref[...]
    grad = grad_ref[...]
    scores = lax.dot_general(query, key, rows_by_rows, preferred_element_type=jnp.float32) * score_scale
    scores = jnp.where(mask_ref[...] > 0, scores, -1e30)
    row_peak = jnp.max(scores, axis=1, keepdims=True)
    exp_scores = jnp.exp(scores - row_peak)
    probs = exp_scores / jnp.sum(exp_scores, axis=1, keepdims=True)
    probs_low = probs.astype(jnp.bfloat16)
    attn = jnp.dot(probs_low, value, preferred_element_type=jnp.float32).astype(jnp.bfloat16)
    attn_ref[...] = attn
    row_delta = jnp.sum(grad.astype(jnp.float32) * attn.astype(jnp.float32), axis=1, keepdims=True)
    dprobs = lax.dot_general(grad, value, rows_by_rows, preferred_element_type=jnp.float32)
    dscores = (probs * (dprobs - row_delta)).astype(jnp.bfloat16)
    dq_ref[...] = (jnp.dot(dscores, key, preferred_element_type=jnp.float32) * score_scale).astype(jnp.bfloat16)
    dk_ref[...] = (
        lax.dot_general(dscores, query, cols_by_cols, preferred_element_type=jnp.float32) * score_scale
    ).astype(jnp.bfloat16)
    dv_ref[...] = lax.dot_general(probs_low, grad, cols_by_cols, preferred_element_type=jnp.float32).astype(jnp.bfloat16)


def body(queries, keys, values, tile_lists, grad_out, w_out):
    query_tile = queries[0, 0]
    key_tile = keys[0, 0]
    value_tile = values[0, 0]
    grad_tile = grad_out[0, 0]
    listed = tile_lists[0]
    tile_tok, inner_width = query_tile.shape
    slot_count = listed.shape[0]
    height_tiles = H_TILES
    score_scale = 1.0 / math.sqrt(HEAD)
    own_tile = lax.axis_index("sp")
    key_value = jnp.stack([key_tile, value_tile])
    def shifted(value, time_step, height_step, toward):
        return neighbour_shift(value, "sp", time_step, height_step, height_tiles, toward)

    earlier = shifted(key_value, -1, 0, False)
    later = shifted(key_value, 1, 0, False)
    column = [earlier, key_value, later]
    relayed = jnp.stack([earlier, later])
    side_own = {step: shifted(key_value, 0, step, False) for step in (-1, 1)}
    side_relayed = {step: shifted(relayed, 0, step, False) for step in (-1, 1)}
    pieces = []
    for time_step in (-1, 0, 1):
        for height_step in (-1, 0, 1):
            if height_step == 0:
                pieces.append(column[time_step + 1])
            elif time_step == 0:
                pieces.append(side_own[height_step])
            else:
                pieces.append(side_relayed[height_step][(time_step + 1) // 2])
    window = jnp.stack(pieces)
    valid_slot = listed >= 0
    time_gap = listed // height_tiles - own_tile // height_tiles
    height_gap = listed % height_tiles - own_tile % height_tiles
    slot_index = jnp.where(valid_slot, (time_gap + 1) * 3 + height_gap + 1, 4)
    picked = jnp.take(window, slot_index, axis=0)
    key_rows = picked[:, 0].reshape(slot_count * tile_tok, inner_width)
    value_rows = picked[:, 1].reshape(slot_count * tile_tok, inner_width)
    key_mask = jnp.repeat(valid_slot, tile_tok)
    grad_attn = lax.dot_general(
        grad_tile, w_out, (((1,), (1,)), ((), ())), preferred_element_type=jnp.float32
    ).astype(jnp.bfloat16)
    key_count = slot_count * tile_tok
    mask_row = key_mask.astype(jnp.int32).reshape(1, key_count)
    head_count = inner_width // HEAD
    tile_spec = pl.BlockSpec((tile_tok, HEAD), lambda head: (0, head))
    key_spec = pl.BlockSpec((key_count, HEAD), lambda head: (0, head))
    attn_all, grad_query, grad_key, grad_value = pl.pallas_call(
        functools.partial(tile_attention, score_scale=score_scale),
        grid=(head_count,),
        in_specs=[
            pl.BlockSpec((1, key_count), lambda head: (0, 0)),
            tile_spec,
            key_spec,
            key_spec,
            tile_spec,
        ],
        out_specs=[tile_spec, tile_spec, key_spec, key_spec],
        out_shape=[
            jax.ShapeDtypeStruct((tile_tok, inner_width), jnp.bfloat16),
            jax.ShapeDtypeStruct((tile_tok, inner_width), jnp.bfloat16),
            jax.ShapeDtypeStruct((key_count, inner_width), jnp.bfloat16),
            jax.ShapeDtypeStruct((key_count, inner_width), jnp.bfloat16),
        ],
        cost_estimate=pl.CostEstimate(
            flops=2 * 5 * tile_tok * key_count * inner_width,
            transcendentals=head_count * tile_tok * key_count,
            bytes_accessed=2 * 2 * (2 * tile_tok + 2 * key_count) * inner_width,
        ),
    )(mask_row, query_tile, key_rows, value_rows, grad_attn)
    dp_count = lax.axis_size("dp")
    sp_count = lax.axis_size("sp")
    dp_index = lax.axis_index("dp")
    core, high = dp_index % 2, dp_index // 2
    row_block = inner_width // dp_count
    model_width = grad_tile.shape[1]
    col_block = model_width // sp_count
    attn_blocks = attn_all.reshape(tile_tok, dp_count // 2, 2, row_block)
    kept_rows = lax.dynamic_index_in_dim(attn_blocks, core, 2, keepdims=False).reshape(tile_tok, -1)
    sent_rows = lax.dynamic_index_in_dim(attn_blocks, 1 - core, 2, keepdims=False).reshape(tile_tok, -1)
    contract_tokens = (((0,), (0,)), ((), ()))
    kept_part = lax.dot_general(grad_tile, kept_rows, contract_tokens, preferred_element_type=jnp.float32)
    sent_part = lax.dot_general(grad_tile, sent_rows, contract_tokens, preferred_element_type=jnp.float32)
    sibling_part = lax.ppermute(
        sent_part.astype(jnp.bfloat16), "dp", [(index, index ^ 1) for index in range(dp_count)]
    )
    core_sum = (kept_part + sibling_part.astype(jnp.float32)).astype(jnp.bfloat16)
    by_column = lax.all_to_all(
        core_sum.reshape(sp_count, col_block, -1), "sp", 0, 0, tiled=True
    )
    column_sum = by_column.astype(jnp.float32).sum(0).reshape(col_block, dp_count // 2, row_block)
    own_half = lax.dynamic_index_in_dim(column_sum, high, 1, keepdims=False)
    other_half = lax.dynamic_index_in_dim(column_sum, 1 - high, 1, keepdims=False)
    weight_grad = (
        own_half
        + lax.ppermute(other_half, "dp", [(index, (index + 2) % dp_count) for index in range(dp_count)])
    ).T
    key_terms = grad_key.reshape(slot_count, tile_tok, inner_width)
    value_terms = grad_value.reshape(slot_count, tile_tok, inner_width)
    matches = (slot_index[:, None] == jnp.arange(9, dtype=jnp.int32)[None, :]) & valid_slot[:, None]
    match_slot = jnp.argmax(matches, axis=0)
    match_any = jnp.any(matches, axis=0)

    def slot_payload(slot_number):
        picked_slot = match_slot[slot_number]
        payload = jnp.stack(
            [
                lax.dynamic_index_in_dim(key_terms, picked_slot, 0, keepdims=False),
                lax.dynamic_index_in_dim(value_terms, picked_slot, 0, keepdims=False),
            ]
        )
        return jnp.where(match_any[slot_number], payload, jnp.zeros_like(payload))

    from_side = {
        step: shifted(
            jnp.stack([slot_payload(time_step * 3 + step + 4) for time_step in (-1, 0, 1)]), 0, step, True
        ).astype(jnp.float32)
        for step in (-1, 1)
    }
    column_sums = [
        slot_payload(time_step * 3 + 4).astype(jnp.float32)
        + from_side[-1][time_step + 1]
        + from_side[1][time_step + 1]
        for time_step in (-1, 0, 1)
    ]
    grad_total = (
        column_sums[1]
        + shifted(column_sums[0].astype(jnp.bfloat16), -1, 0, True).astype(jnp.float32)
        + shifted(column_sums[2].astype(jnp.bfloat16), 1, 0, True).astype(jnp.float32)
    )
    grad_kv = grad_total.astype(jnp.bfloat16)
    return (grad_query[None, None], grad_kv[0][None, None], grad_kv[1][None, None], weight_grad)


def solution(mesh):
    in_specs = (
        P("dp", "sp", None, None),
        P("dp", "sp", None, None),
        P("dp", "sp", None, None),
        P("sp", None),
        P("dp", "sp", None, None),
        P(),
    )
    out_specs = (
        P("dp", "sp", None, None),
        P("dp", "sp", None, None),
        P("dp", "sp", None, None),
        P("dp", "sp"),
    )
    return jax.shard_map(body, mesh=mesh, in_specs=in_specs, out_specs=out_specs, check_vma=False)
```

```python
import functools
import math

import jax
import jax.numpy as jnp
from jax import lax
from jax.experimental import pallas as pl
from jax.sharding import PartitionSpec as P

HEAD = 128
H_TILES = 4


def neighbour_shift(value, axis, time_step, height_step, height_tiles, toward):
    count = lax.axis_size(axis)
    time_tiles = count // height_tiles
    offset = time_step * height_tiles + height_step
    pairs = []
    for tile in range(count):
        time_row, height_col = divmod(tile, height_tiles)
        if 0 <= time_row + time_step < time_tiles and 0 <= height_col + height_step < height_tiles:
            pairs.append((tile, tile + offset) if toward else (tile + offset, tile))
    return lax.ppermute(value, axis, pairs)


def tile_attention(mask_ref, query_ref, key_ref, value_ref, grad_ref, attn_ref, dq_ref, dk_ref, dv_ref, *, score_scale):
    rows_by_rows = (((1,), (1,)), ((), ()))
    cols_by_cols = (((0,), (0,)), ((), ()))
    query = query_ref[...]
    key = key_ref[...]
    value = value_ref[...]
    grad = grad_ref[...]
    scores = lax.dot_general(query, key, rows_by_rows, preferred_element_type=jnp.float32) * score_scale
    scores = jnp.where(mask_ref[...] > 0, scores, -1e30)
    row_peak = jnp.max(scores, axis=1, keepdims=True)
    exp_scores = jnp.exp(scores - row_peak)
    probs = exp_scores / jnp.sum(exp_scores, axis=1, keepdims=True)
    probs_low = probs.astype(jnp.bfloat16)
    attn = jnp.dot(probs_low, value, preferred_element_type=jnp.float32).astype(jnp.bfloat16)
    attn_ref[...] = attn
    row_delta = jnp.sum(grad.astype(jnp.float32) * attn.astype(jnp.float32), axis=1, keepdims=True)
    dprobs = lax.dot_general(grad, value, rows_by_rows, preferred_element_type=jnp.float32)
    dscores = (probs * (dprobs - row_delta)).astype(jnp.bfloat16)
    dq_ref[...] = (jnp.dot(dscores, key, preferred_element_type=jnp.float32) * score_scale).astype(jnp.bfloat16)
    dk_ref[...] = (
        lax.dot_general(dscores, query, cols_by_cols, preferred_element_type=jnp.float32) * score_scale
    ).astype(jnp.bfloat16)
    dv_ref[...] = lax.dot_general(probs_low, grad, cols_by_cols, preferred_element_type=jnp.float32).astype(jnp.bfloat16)


def body(queries, keys, values, tile_lists, grad_out, w_out):
    query_tile = queries[0, 0]
    key_tile = keys[0, 0]
    value_tile = values[0, 0]
    grad_tile = grad_out[0, 0]
    listed = tile_lists[0]
    tile_tok, inner_width = query_tile.shape
    slot_count = listed.shape[0]
    height_tiles = H_TILES
    score_scale = 1.0 / math.sqrt(HEAD)
    own_tile = lax.axis_index("sp")
    key_value = jnp.stack([key_tile, value_tile])
    def shifted(value, time_step, height_step, toward):
        return neighbour_shift(value, "sp", time_step, height_step, height_tiles, toward)

    earlier, later, left_own, right_own = lax.optimization_barrier(
        (
            shifted(key_value, -1, 0, False),
            shifted(key_value, 1, 0, False),
            shifted(key_value, 0, -1, False),
            shifted(key_value, 0, 1, False),
        )
    )
    column = [earlier, key_value, later]
    relayed = jnp.stack([earlier, later])
    side_own = {-1: left_own, 1: right_own}
    side_relayed = {step: shifted(relayed, 0, step, False) for step in (-1, 1)}
    pieces = []
    for time_step in (-1, 0, 1):
        for height_step in (-1, 0, 1):
            if height_step == 0:
                pieces.append(column[time_step + 1])
            elif time_step == 0:
                pieces.append(side_own[height_step])
            else:
                pieces.append(side_relayed[height_step][(time_step + 1) // 2])
    window = jnp.stack(pieces)
    valid_slot = listed >= 0
    time_gap = listed // height_tiles - own_tile // height_tiles
    height_gap = listed % height_tiles - own_tile % height_tiles
    slot_index = jnp.where(valid_slot, (time_gap + 1) * 3 + height_gap + 1, 4)
    picked = jnp.take(window, slot_index, axis=0)
    key_rows = picked[:, 0].reshape(slot_count * tile_tok, inner_width)
    value_rows = picked[:, 1].reshape(slot_count * tile_tok, inner_width)
    key_mask = jnp.repeat(valid_slot, tile_tok)
    grad_attn = lax.dot_general(
        grad_tile, w_out, (((1,), (1,)), ((), ())), preferred_element_type=jnp.float32
    ).astype(jnp.bfloat16)
    key_count = slot_count * tile_tok
    mask_row = key_mask.astype(jnp.int32).reshape(1, key_count)
    head_count = inner_width // HEAD
    tile_spec = pl.BlockSpec((tile_tok, HEAD), lambda head: (0, head))
    key_spec = pl.BlockSpec((key_count, HEAD), lambda head: (0, head))
    attn_all, grad_query, grad_key, grad_value = pl.pallas_call(
        functools.partial(tile_attention, score_scale=score_scale),
        grid=(head_count,),
        in_specs=[
            pl.BlockSpec((1, key_count), lambda head: (0, 0)),
            tile_spec,
            key_spec,
            key_spec,
            tile_spec,
        ],
        out_specs=[tile_spec, tile_spec, key_spec, key_spec],
        out_shape=[
            jax.ShapeDtypeStruct((tile_tok, inner_width), jnp.bfloat16),
            jax.ShapeDtypeStruct((tile_tok, inner_width), jnp.bfloat16),
            jax.ShapeDtypeStruct((key_count, inner_width), jnp.bfloat16),
            jax.ShapeDtypeStruct((key_count, inner_width), jnp.bfloat16),
        ],
        cost_estimate=pl.CostEstimate(
            flops=2 * 5 * tile_tok * key_count * inner_width,
            transcendentals=head_count * tile_tok * key_count,
            bytes_accessed=2 * 2 * (2 * tile_tok + 2 * key_count) * inner_width,
        ),
    )(mask_row, query_tile, key_rows, value_rows, grad_attn)
    dp_count = lax.axis_size("dp")
    sp_count = lax.axis_size("sp")
    dp_index = lax.axis_index("dp")
    core, high = dp_index % 2, dp_index // 2
    row_block = inner_width // dp_count
    model_width = grad_tile.shape[1]
    col_block = model_width // sp_count
    attn_blocks = attn_all.reshape(tile_tok, dp_count // 2, 2, row_block)
    kept_rows = lax.dynamic_index_in_dim(attn_blocks, core, 2, keepdims=False).reshape(tile_tok, -1)
    sent_rows = lax.dynamic_index_in_dim(attn_blocks, 1 - core, 2, keepdims=False).reshape(tile_tok, -1)
    contract_tokens = (((0,), (0,)), ((), ()))
    kept_part = lax.dot_general(grad_tile, kept_rows, contract_tokens, preferred_element_type=jnp.float32)
    sent_part = lax.dot_general(grad_tile, sent_rows, contract_tokens, preferred_element_type=jnp.float32)
    sibling_part = lax.ppermute(
        sent_part.astype(jnp.bfloat16), "dp", [(index, index ^ 1) for index in range(dp_count)]
    )
    core_sum = (kept_part + sibling_part.astype(jnp.float32)).astype(jnp.bfloat16)
    by_column = lax.all_to_all(
        core_sum.reshape(sp_count, col_block, -1), "sp", 0, 0, tiled=True
    )
    column_sum = by_column.astype(jnp.float32).sum(0).reshape(col_block, dp_count // 2, row_block)
    own_half = lax.dynamic_index_in_dim(column_sum, high, 1, keepdims=False)
    other_half = lax.dynamic_index_in_dim(column_sum, 1 - high, 1, keepdims=False)
    weight_grad = (
        own_half
        + lax.ppermute(other_half, "dp", [(index, (index + 2) % dp_count) for index in range(dp_count)])
    ).T
    key_terms = grad_key.reshape(slot_count, tile_tok, inner_width)
    value_terms = grad_value.reshape(slot_count, tile_tok, inner_width)
    matches = (slot_index[:, None] == jnp.arange(9, dtype=jnp.int32)[None, :]) & valid_slot[:, None]
    match_slot = jnp.argmax(matches, axis=0)
    match_any = jnp.any(matches, axis=0)

    def slot_payload(slot_number):
        picked_slot = match_slot[slot_number]
        payload = jnp.stack(
            [
                lax.dynamic_index_in_dim(key_terms, picked_slot, 0, keepdims=False),
                lax.dynamic_index_in_dim(value_terms, picked_slot, 0, keepdims=False),
            ]
        )
        return jnp.where(match_any[slot_number], payload, jnp.zeros_like(payload))

    diagonal_sends = [
        shifted(jnp.stack([slot_payload(step + 1), slot_payload(step + 7)]), 0, step, True)
        for step in (-1, 1)
    ]
    own_row_parts = [slot_payload(step + 4) for step in (-1, 1)]
    diagonal_in, own_row_parts = lax.optimization_barrier((diagonal_sends, own_row_parts))
    diagonal_in = [part.astype(jnp.float32) for part in diagonal_in]
    row_in = [
        shifted(part, 0, step, True).astype(jnp.float32)
        for part, step in zip(own_row_parts, (-1, 1))
    ]
    earlier_sum = slot_payload(1).astype(jnp.float32) + diagonal_in[0][0] + diagonal_in[1][0]
    later_sum = slot_payload(7).astype(jnp.float32) + diagonal_in[0][1] + diagonal_in[1][1]
    grad_total = (
        slot_payload(4).astype(jnp.float32)
        + row_in[0]
        + row_in[1]
        + shifted(earlier_sum.astype(jnp.bfloat16), -1, 0, True).astype(jnp.float32)
        + shifted(later_sum.astype(jnp.bfloat16), 1, 0, True).astype(jnp.float32)
    )
    grad_kv = grad_total.astype(jnp.bfloat16)
    return (grad_query[None, None], grad_kv[0][None, None], grad_kv[1][None, None], weight_grad)


def solution(mesh):
    in_specs = (
        P("dp", "sp", None, None),
        P("dp", "sp", None, None),
        P("dp", "sp", None, None),
        P("sp", None),
        P("dp", "sp", None, None),
        P(),
    )
    out_specs = (
        P("dp", "sp", None, None),
        P("dp", "sp", None, None),
        P("dp", "sp", None, None),
        P("dp", "sp"),
    )
    return jax.shard_map(body, mesh=mesh, in_specs=in_specs, out_specs=out_specs, check_vma=False)
```

```python
import functools
import math

import jax
import jax.numpy as jnp
from jax import lax
from jax.experimental import pallas as pl
from jax.sharding import PartitionSpec as P

HEAD = 128
H_TILES = 4


def neighbour_shift(value, axis, time_step, height_step, height_tiles, toward):
    count = lax.axis_size(axis)
    time_tiles = count // height_tiles
    offset = time_step * height_tiles + height_step
    pairs = []
    for tile in range(count):
        time_row, height_col = divmod(tile, height_tiles)
        if 0 <= time_row + time_step < time_tiles and 0 <= height_col + height_step < height_tiles:
            pairs.append((tile, tile + offset) if toward else (tile + offset, tile))
    return lax.ppermute(value, axis, pairs)


def tile_attention(mask_ref, query_ref, grad_ref, *refs, score_scale):
    in_refs, out_refs = refs[:7], refs[7:]
    attn_ref, dq_ref = out_refs[:2]

    def by_direction(group):
        earlier, own, later, left, right, rel_left, rel_right = group
        return [
            (rel_left, 0), (earlier, None), (rel_right, 0),
            (left, None), (own, None), (right, None),
            (rel_left, 1), (later, None), (rel_right, 1),
        ]

    def read(ref, pair, part):
        return ref[part] if pair is None else ref[pair, part]

    def write(ref, pair, part, block):
        if pair is None:
            ref[part] = block
        else:
            ref[pair, part] = block

    directions = by_direction(in_refs)
    out_directions = by_direction(out_refs[2:])
    rows_by_rows = (((1,), (1,)), ((), ()))
    cols_by_cols = (((0,), (0,)), ((), ()))
    query = query_ref[...]
    grad = grad_ref[...]
    key = jnp.concatenate([read(ref, pair, 0) for ref, pair in directions], axis=0)
    value = jnp.concatenate([read(ref, pair, 1) for ref, pair in directions], axis=0)
    scores = lax.dot_general(query, key, rows_by_rows, preferred_element_type=jnp.float32) * score_scale
    scores = jnp.where(mask_ref[...] > 0, scores, -1e30)
    row_peak = jnp.max(scores, axis=1, keepdims=True)
    exp_scores = jnp.exp(scores - row_peak)
    probs = exp_scores / jnp.sum(exp_scores, axis=1, keepdims=True)
    probs_low = probs.astype(jnp.bfloat16)
    attn = jnp.dot(probs_low, value, preferred_element_type=jnp.float32).astype(jnp.bfloat16)
    attn_ref[...] = attn
    row_delta = jnp.sum(grad.astype(jnp.float32) * attn.astype(jnp.float32), axis=1, keepdims=True)
    dprobs = lax.dot_general(grad, value, rows_by_rows, preferred_element_type=jnp.float32)
    dscores = (probs * (dprobs - row_delta)).astype(jnp.bfloat16)
    dq_ref[...] = (jnp.dot(dscores, key, preferred_element_type=jnp.float32) * score_scale).astype(jnp.bfloat16)
    grad_key = (
        lax.dot_general(dscores, query, cols_by_cols, preferred_element_type=jnp.float32) * score_scale
    ).astype(jnp.bfloat16)
    grad_value = lax.dot_general(probs_low, grad, cols_by_cols, preferred_element_type=jnp.float32).astype(jnp.bfloat16)
    tile_tok = query.shape[0]
    for number, (ref, pair) in enumerate(out_directions):
        rows = slice(number * tile_tok, (number + 1) * tile_tok)
        write(ref, pair, 0, grad_key[rows])
        write(ref, pair, 1, grad_value[rows])


def body(queries, keys, values, tile_lists, grad_out, w_out):
    query_tile = queries[0, 0]
    key_tile = keys[0, 0]
    value_tile = values[0, 0]
    grad_tile = grad_out[0, 0]
    listed = tile_lists[0]
    tile_tok, inner_width = query_tile.shape
    slot_count = listed.shape[0]
    height_tiles = H_TILES
    score_scale = 1.0 / math.sqrt(HEAD)
    own_tile = lax.axis_index("sp")
    key_value = jnp.stack([key_tile, value_tile])
    def shifted(value, time_step, height_step, toward):
        return neighbour_shift(value, "sp", time_step, height_step, height_tiles, toward)

    earlier, later, left_own, right_own = lax.optimization_barrier(
        (
            shifted(key_value, -1, 0, False),
            shifted(key_value, 1, 0, False),
            shifted(key_value, 0, -1, False),
            shifted(key_value, 0, 1, False),
        )
    )
    relayed = jnp.stack([earlier, later])
    side_relayed = {step: shifted(relayed, 0, step, False) for step in (-1, 1)}
    valid_slot = listed >= 0
    time_gap = listed // height_tiles - own_tile // height_tiles
    height_gap = listed % height_tiles - own_tile % height_tiles
    slot_index = jnp.where(valid_slot, (time_gap + 1) * 3 + height_gap + 1, 4)
    direction_count = 9
    listed_direction = jnp.any(
        (slot_index[:, None] == jnp.arange(direction_count, dtype=jnp.int32)[None, :]) & valid_slot[:, None],
        axis=0,
    )
    key_count = direction_count * tile_tok
    mask_row = jnp.repeat(listed_direction, tile_tok).astype(jnp.int32).reshape(1, key_count)
    grad_attn = lax.dot_general(
        grad_tile, w_out, (((1,), (1,)), ((), ())), preferred_element_type=jnp.float32
    ).astype(jnp.bfloat16)
    head_count = inner_width // HEAD
    tile_spec = pl.BlockSpec((tile_tok, HEAD), lambda head: (0, head))
    single_spec = pl.BlockSpec((2, tile_tok, HEAD), lambda head: (0, 0, head))
    pair_spec = pl.BlockSpec((2, 2, tile_tok, HEAD), lambda head: (0, 0, 0, head))
    group_specs = [single_spec] * 5 + [pair_spec] * 2
    single_shape = jax.ShapeDtypeStruct((2, tile_tok, inner_width), jnp.bfloat16)
    pair_shape = jax.ShapeDtypeStruct((2, 2, tile_tok, inner_width), jnp.bfloat16)
    tile_shape = jax.ShapeDtypeStruct((tile_tok, inner_width), jnp.bfloat16)
    outputs = pl.pallas_call(
        functools.partial(tile_attention, score_scale=score_scale),
        grid=(head_count,),
        in_specs=[pl.BlockSpec((1, key_count), lambda head: (0, 0)), tile_spec, tile_spec, *group_specs],
        out_specs=[tile_spec, tile_spec, *group_specs],
        out_shape=[tile_shape, tile_shape, *[single_shape] * 5, *[pair_shape] * 2],
        cost_estimate=pl.CostEstimate(
            flops=2 * 5 * tile_tok * key_count * inner_width,
            transcendentals=head_count * tile_tok * key_count,
            bytes_accessed=2 * 2 * (2 * tile_tok + 2 * key_count) * inner_width,
        ),
    )(
        mask_row,
        query_tile,
        grad_attn,
        earlier,
        key_value,
        later,
        left_own,
        right_own,
        side_relayed[-1],
        side_relayed[1],
    )
    attn_all, grad_query = outputs[:2]
    back_earlier, back_own, back_later, back_left, back_right, back_rel_left, back_rel_right = outputs[2:]
    dp_count = lax.axis_size("dp")
    sp_count = lax.axis_size("sp")
    dp_index = lax.axis_index("dp")
    core, high = dp_index % 2, dp_index // 2
    row_block = inner_width // dp_count
    model_width = grad_tile.shape[1]
    col_block = model_width // sp_count
    attn_blocks = attn_all.reshape(tile_tok, dp_count // 2, 2, row_block)
    kept_rows = lax.dynamic_index_in_dim(attn_blocks, core, 2, keepdims=False).reshape(tile_tok, -1)
    sent_rows = lax.dynamic_index_in_dim(attn_blocks, 1 - core, 2, keepdims=False).reshape(tile_tok, -1)
    contract_tokens = (((0,), (0,)), ((), ()))
    kept_part = lax.dot_general(grad_tile, kept_rows, contract_tokens, preferred_element_type=jnp.float32)
    sent_part = lax.dot_general(grad_tile, sent_rows, contract_tokens, preferred_element_type=jnp.float32)
    sibling_part = lax.ppermute(
        sent_part.astype(jnp.bfloat16), "dp", [(index, index ^ 1) for index in range(dp_count)]
    )
    core_sum = (kept_part + sibling_part.astype(jnp.float32)).astype(jnp.bfloat16)
    by_column = lax.all_to_all(
        core_sum.reshape(sp_count, col_block, -1), "sp", 0, 0, tiled=True
    )
    column_sum = by_column.astype(jnp.float32).sum(0).reshape(col_block, dp_count // 2, row_block)
    own_half = lax.dynamic_index_in_dim(column_sum, high, 1, keepdims=False)
    other_half = lax.dynamic_index_in_dim(column_sum, 1 - high, 1, keepdims=False)
    weight_grad = (
        own_half
        + lax.ppermute(other_half, "dp", [(index, (index + 2) % dp_count) for index in range(dp_count)])
    ).T
    diagonal_sends = [shifted(back_rel_left, 0, -1, True), shifted(back_rel_right, 0, 1, True)]
    diagonal_in, own_row_parts = lax.optimization_barrier((diagonal_sends, [back_left, back_right]))
    diagonal_in = [part.astype(jnp.float32) for part in diagonal_in]
    row_in = [
        shifted(part, 0, step, True).astype(jnp.float32)
        for part, step in zip(own_row_parts, (-1, 1))
    ]
    earlier_sum = back_earlier.astype(jnp.float32) + diagonal_in[0][0] + diagonal_in[1][0]
    later_sum = back_later.astype(jnp.float32) + diagonal_in[0][1] + diagonal_in[1][1]
    grad_total = (
        back_own.astype(jnp.float32)
        + row_in[0]
        + row_in[1]
        + shifted(earlier_sum.astype(jnp.bfloat16), -1, 0, True).astype(jnp.float32)
        + shifted(later_sum.astype(jnp.bfloat16), 1, 0, True).astype(jnp.float32)
    )
    grad_kv = grad_total.astype(jnp.bfloat16)
    return (grad_query[None, None], grad_kv[0][None, None], grad_kv[1][None, None], weight_grad)


def solution(mesh):
    in_specs = (
        P("dp", "sp", None, None),
        P("dp", "sp", None, None),
        P("dp", "sp", None, None),
        P("sp", None),
        P("dp", "sp", None, None),
        P(),
    )
    out_specs = (
        P("dp", "sp", None, None),
        P("dp", "sp", None, None),
        P("dp", "sp", None, None),
        P("dp", "sp"),
    )
    return jax.shard_map(body, mesh=mesh, in_specs=in_specs, out_specs=out_specs, check_vma=False)
```

```python
import functools
import math

import jax
import jax.numpy as jnp
from jax import lax
from jax.experimental import pallas as pl
from jax.sharding import PartitionSpec as P

HEAD = 128
H_TILES = 4


def neighbour_shift(value, axis, time_step, height_step, height_tiles, toward):
    count = lax.axis_size(axis)
    time_tiles = count // height_tiles
    offset = time_step * height_tiles + height_step
    pairs = []
    for tile in range(count):
        time_row, height_col = divmod(tile, height_tiles)
        if 0 <= time_row + time_step < time_tiles and 0 <= height_col + height_step < height_tiles:
            pairs.append((tile, tile + offset) if toward else (tile + offset, tile))
    return lax.ppermute(value, axis, pairs)


def tile_attention(mask_ref, query_ref, grad_ref, *refs, score_scale):
    directions = refs[:9]
    attn_ref, dq_ref = refs[9:11]
    out_directions = refs[11:]
    rows_by_rows = (((1,), (1,)), ((), ()))
    cols_by_cols = (((0,), (0,)), ((), ()))
    query = query_ref[...]
    grad = grad_ref[...]
    key = jnp.concatenate([ref[0] for ref in directions], axis=0)
    value = jnp.concatenate([ref[1] for ref in directions], axis=0)
    scores = lax.dot_general(query, key, rows_by_rows, preferred_element_type=jnp.float32) * score_scale
    scores = jnp.where(mask_ref[...] > 0, scores, -1e30)
    row_peak = jnp.max(scores, axis=1, keepdims=True)
    exp_scores = jnp.exp(scores - row_peak)
    probs = exp_scores / jnp.sum(exp_scores, axis=1, keepdims=True)
    probs_low = probs.astype(jnp.bfloat16)
    attn = jnp.dot(probs_low, value, preferred_element_type=jnp.float32).astype(jnp.bfloat16)
    attn_ref[...] = attn
    row_delta = jnp.sum(grad.astype(jnp.float32) * attn.astype(jnp.float32), axis=1, keepdims=True)
    dprobs = lax.dot_general(grad, value, rows_by_rows, preferred_element_type=jnp.float32)
    dscores = (probs * (dprobs - row_delta)).astype(jnp.bfloat16)
    dq_ref[...] = (jnp.dot(dscores, key, preferred_element_type=jnp.float32) * score_scale).astype(jnp.bfloat16)
    grad_key = (
        lax.dot_general(dscores, query, cols_by_cols, preferred_element_type=jnp.float32) * score_scale
    ).astype(jnp.bfloat16)
    grad_value = lax.dot_general(probs_low, grad, cols_by_cols, preferred_element_type=jnp.float32).astype(jnp.bfloat16)
    tile_tok = query.shape[0]
    for number, ref in enumerate(out_directions):
        rows = slice(number * tile_tok, (number + 1) * tile_tok)
        ref[0] = grad_key[rows]
        ref[1] = grad_value[rows]


def body(queries, keys, values, tile_lists, grad_out, w_out):
    query_tile = queries[0, 0]
    key_tile = keys[0, 0]
    value_tile = values[0, 0]
    grad_tile = grad_out[0, 0]
    listed = tile_lists[0]
    tile_tok, inner_width = query_tile.shape
    slot_count = listed.shape[0]
    height_tiles = H_TILES
    score_scale = 1.0 / math.sqrt(HEAD)
    own_tile = lax.axis_index("sp")
    key_value = jnp.stack([key_tile, value_tile])
    def shifted(value, time_step, height_step, toward):
        return neighbour_shift(value, "sp", time_step, height_step, height_tiles, toward)

    earlier, left_own, right_own = lax.optimization_barrier(
        (
            shifted(key_value, -1, 0, False),
            shifted(key_value, 0, -1, False),
            shifted(key_value, 0, 1, False),
        )
    )
    later = shifted(key_value, 1, 0, False)
    gathered = [
        shifted(earlier, 0, -1, False), earlier, shifted(earlier, 0, 1, False),
        left_own, key_value, right_own,
        shifted(later, 0, -1, False), later, shifted(later, 0, 1, False),
    ]
    valid_slot = listed >= 0
    time_gap = listed // height_tiles - own_tile // height_tiles
    height_gap = listed % height_tiles - own_tile % height_tiles
    slot_index = jnp.where(valid_slot, (time_gap + 1) * 3 + height_gap + 1, 4)
    direction_count = 9
    listed_direction = jnp.any(
        (slot_index[:, None] == jnp.arange(direction_count, dtype=jnp.int32)[None, :]) & valid_slot[:, None],
        axis=0,
    )
    key_count = direction_count * tile_tok
    mask_row = jnp.repeat(listed_direction, tile_tok).astype(jnp.int32).reshape(1, key_count)
    grad_attn = lax.dot_general(
        grad_tile, w_out, (((1,), (1,)), ((), ())), preferred_element_type=jnp.float32
    ).astype(jnp.bfloat16)
    head_count = inner_width // HEAD
    tile_spec = pl.BlockSpec((tile_tok, HEAD), lambda head: (0, head))
    single_spec = pl.BlockSpec((2, tile_tok, HEAD), lambda head: (0, 0, head))
    single_shape = jax.ShapeDtypeStruct((2, tile_tok, inner_width), jnp.bfloat16)
    tile_shape = jax.ShapeDtypeStruct((tile_tok, inner_width), jnp.bfloat16)
    outputs = pl.pallas_call(
        functools.partial(tile_attention, score_scale=score_scale),
        grid=(head_count,),
        in_specs=[pl.BlockSpec((1, key_count), lambda head: (0, 0)), tile_spec, tile_spec, *[single_spec] * direction_count],
        out_specs=[tile_spec, tile_spec, *[single_spec] * direction_count],
        out_shape=[tile_shape, tile_shape, *[single_shape] * direction_count],
        cost_estimate=pl.CostEstimate(
            flops=2 * 5 * tile_tok * key_count * inner_width,
            transcendentals=head_count * tile_tok * key_count,
            bytes_accessed=2 * 2 * (2 * tile_tok + 2 * key_count) * inner_width,
        ),
    )(
        mask_row,
        query_tile,
        grad_attn,
        *gathered,
    )
    attn_all, grad_query = outputs[:2]
    back = outputs[2:]
    dp_count = lax.axis_size("dp")
    sp_count = lax.axis_size("sp")
    dp_index = lax.axis_index("dp")
    core, high = dp_index % 2, dp_index // 2
    row_block = inner_width // dp_count
    model_width = grad_tile.shape[1]
    col_block = model_width // sp_count
    attn_blocks = attn_all.reshape(tile_tok, dp_count // 2, 2, row_block)
    kept_rows = lax.dynamic_index_in_dim(attn_blocks, core, 2, keepdims=False).reshape(tile_tok, -1)
    sent_rows = lax.dynamic_index_in_dim(attn_blocks, 1 - core, 2, keepdims=False).reshape(tile_tok, -1)
    contract_tokens = (((0,), (0,)), ((), ()))
    kept_part = lax.dot_general(grad_tile, kept_rows, contract_tokens, preferred_element_type=jnp.float32)
    sent_part = lax.dot_general(grad_tile, sent_rows, contract_tokens, preferred_element_type=jnp.float32)
    sibling_part = lax.ppermute(
        sent_part.astype(jnp.bfloat16), "dp", [(index, index ^ 1) for index in range(dp_count)]
    )
    core_sum = (kept_part + sibling_part.astype(jnp.float32)).astype(jnp.bfloat16)
    by_column = lax.all_to_all(
        core_sum.reshape(sp_count, col_block, -1), "sp", 0, 0, tiled=True
    )
    column_sum = by_column.astype(jnp.float32).sum(0).reshape(col_block, dp_count // 2, row_block)
    own_half = lax.dynamic_index_in_dim(column_sum, high, 1, keepdims=False)
    other_half = lax.dynamic_index_in_dim(column_sum, 1 - high, 1, keepdims=False)
    weight_grad = (
        own_half
        + lax.ppermute(other_half, "dp", [(index, (index + 2) % dp_count) for index in range(dp_count)])
    ).T
    early_in = [shifted(back[0], 0, -1, True), shifted(back[2], 0, 1, True)]
    early_in, late_out, row_out = lax.optimization_barrier((early_in, [back[6], back[8]], [back[3], back[5]]))
    earlier_sum = back[1].astype(jnp.float32) + early_in[0].astype(jnp.float32) + early_in[1].astype(jnp.float32)
    from_later = shifted(earlier_sum.astype(jnp.bfloat16), -1, 0, True)
    late_in = [shifted(late_out[0], 0, -1, True), shifted(late_out[1], 0, 1, True)]
    row_in = [shifted(part, 0, step, True) for part, step in zip(row_out, (-1, 1))]
    later_sum = back[7].astype(jnp.float32) + late_in[0].astype(jnp.float32) + late_in[1].astype(jnp.float32)
    from_earlier = shifted(later_sum.astype(jnp.bfloat16), 1, 0, True)
    grad_total = (
        back[4].astype(jnp.float32)
        + row_in[0].astype(jnp.float32)
        + row_in[1].astype(jnp.float32)
        + from_later.astype(jnp.float32)
        + from_earlier.astype(jnp.float32)
    )
    grad_kv = grad_total.astype(jnp.bfloat16)
    return (grad_query[None, None], grad_kv[0][None, None], grad_kv[1][None, None], weight_grad)


def solution(mesh):
    in_specs = (
        P("dp", "sp", None, None),
        P("dp", "sp", None, None),
        P("dp", "sp", None, None),
        P("sp", None),
        P("dp", "sp", None, None),
        P(),
    )
    out_specs = (
        P("dp", "sp", None, None),
        P("dp", "sp", None, None),
        P("dp", "sp", None, None),
        P("dp", "sp"),
    )
    return jax.shard_map(body, mesh=mesh, in_specs=in_specs, out_specs=out_specs, check_vma=False)
```

```python
import functools
import math

import jax
import jax.numpy as jnp
from jax import lax
from jax.experimental import pallas as pl
from jax.sharding import PartitionSpec as P

HEAD = 128
H_TILES = 4


def neighbour_shift(value, axis, time_step, height_step, height_tiles, toward):
    count = lax.axis_size(axis)
    time_tiles = count // height_tiles
    offset = time_step * height_tiles + height_step
    pairs = []
    for tile in range(count):
        time_row, height_col = divmod(tile, height_tiles)
        if 0 <= time_row + time_step < time_tiles and 0 <= height_col + height_step < height_tiles:
            pairs.append((tile, tile + offset) if toward else (tile + offset, tile))
    return lax.ppermute(value, axis, pairs)


def tile_attention(mask_ref, query_ref, grad_ref, *refs, score_scale):
    directions = refs[:9]
    attn_ref, dq_ref = refs[9:11]
    out_directions = refs[11:]
    rows_by_rows = (((1,), (1,)), ((), ()))
    cols_by_cols = (((0,), (0,)), ((), ()))
    query = query_ref[...]
    grad = grad_ref[...]
    key = jnp.concatenate([ref[0] for ref in directions], axis=0)
    value = jnp.concatenate([ref[1] for ref in directions], axis=0)
    scores = lax.dot_general(query, key, rows_by_rows, preferred_element_type=jnp.float32) * score_scale
    scores = jnp.where(mask_ref[...] > 0, scores, -1e30)
    row_peak = jnp.max(scores, axis=1, keepdims=True)
    exp_scores = jnp.exp(scores - row_peak)
    probs = exp_scores / jnp.sum(exp_scores, axis=1, keepdims=True)
    probs_low = probs.astype(jnp.bfloat16)
    attn = jnp.dot(probs_low, value, preferred_element_type=jnp.float32).astype(jnp.bfloat16)
    attn_ref[...] = attn
    row_delta = jnp.sum(grad.astype(jnp.float32) * attn.astype(jnp.float32), axis=1, keepdims=True)
    dprobs = lax.dot_general(grad, value, rows_by_rows, preferred_element_type=jnp.float32)
    dscores = (probs * (dprobs - row_delta)).astype(jnp.bfloat16)
    dq_ref[...] = (jnp.dot(dscores, key, preferred_element_type=jnp.float32) * score_scale).astype(jnp.bfloat16)
    grad_key = (
        lax.dot_general(dscores, query, cols_by_cols, preferred_element_type=jnp.float32) * score_scale
    ).astype(jnp.bfloat16)
    grad_value = lax.dot_general(probs_low, grad, cols_by_cols, preferred_element_type=jnp.float32).astype(jnp.bfloat16)
    tile_tok = query.shape[0]
    for number, ref in enumerate(out_directions):
        rows = slice(number * tile_tok, (number + 1) * tile_tok)
        ref[0] = grad_key[rows]
        ref[1] = grad_value[rows]


def body(queries, keys, values, tile_lists, grad_out, w_out):
    query_tile = queries[0, 0]
    key_tile = keys[0, 0]
    value_tile = values[0, 0]
    grad_tile = grad_out[0, 0]
    listed = tile_lists[0]
    tile_tok, inner_width = query_tile.shape
    slot_count = listed.shape[0]
    height_tiles = H_TILES
    score_scale = 1.0 / math.sqrt(HEAD)
    own_tile = lax.axis_index("sp")
    key_value = jnp.stack([key_tile, value_tile])
    def shifted(value, time_step, height_step, toward):
        return neighbour_shift(value, "sp", time_step, height_step, height_tiles, toward)

    earlier, left_own, right_own = lax.optimization_barrier(
        (
            shifted(key_value, -1, 0, False),
            shifted(key_value, 0, -1, False),
            shifted(key_value, 0, 1, False),
        )
    )
    later = shifted(key_value, 1, 0, False)
    gathered = [
        shifted(earlier, 0, -1, False), earlier, shifted(earlier, 0, 1, False),
        left_own, key_value, right_own,
        shifted(later, 0, -1, False), later, shifted(later, 0, 1, False),
    ]
    valid_slot = listed >= 0
    time_gap = listed // height_tiles - own_tile // height_tiles
    height_gap = listed % height_tiles - own_tile % height_tiles
    slot_index = jnp.where(valid_slot, (time_gap + 1) * 3 + height_gap + 1, 4)
    direction_count = 9
    listed_direction = jnp.any(
        (slot_index[:, None] == jnp.arange(direction_count, dtype=jnp.int32)[None, :]) & valid_slot[:, None],
        axis=0,
    )
    key_count = direction_count * tile_tok
    mask_row = jnp.repeat(listed_direction, tile_tok).astype(jnp.int32).reshape(1, key_count)
    grad_attn = lax.dot_general(
        grad_tile, w_out, (((1,), (1,)), ((), ())), preferred_element_type=jnp.float32
    ).astype(jnp.bfloat16)
    head_count = inner_width // HEAD
    tile_spec = pl.BlockSpec((tile_tok, HEAD), lambda head: (0, head))
    single_spec = pl.BlockSpec((2, tile_tok, HEAD), lambda head: (0, 0, head))
    single_shape = jax.ShapeDtypeStruct((2, tile_tok, inner_width), jnp.bfloat16)
    tile_shape = jax.ShapeDtypeStruct((tile_tok, inner_width), jnp.bfloat16)
    outputs = pl.pallas_call(
        functools.partial(tile_attention, score_scale=score_scale),
        grid=(head_count,),
        in_specs=[pl.BlockSpec((1, key_count), lambda head: (0, 0)), tile_spec, tile_spec, *[single_spec] * direction_count],
        out_specs=[tile_spec, tile_spec, *[single_spec] * direction_count],
        out_shape=[tile_shape, tile_shape, *[single_shape] * direction_count],
        cost_estimate=pl.CostEstimate(
            flops=2 * 5 * tile_tok * key_count * inner_width,
            transcendentals=head_count * tile_tok * key_count,
            bytes_accessed=2 * 2 * (2 * tile_tok + 2 * key_count) * inner_width,
        ),
    )(
        mask_row,
        query_tile,
        grad_attn,
        *gathered,
    )
    attn_all, grad_query = outputs[:2]
    back = outputs[2:]
    early_in = [shifted(back[0], 0, -1, True), shifted(back[2], 0, 1, True)]
    early_in, late_out, row_out = lax.optimization_barrier((early_in, [back[6], back[8]], [back[3], back[5]]))
    earlier_sum = back[1].astype(jnp.float32) + early_in[0].astype(jnp.float32) + early_in[1].astype(jnp.float32)
    from_later = shifted(earlier_sum.astype(jnp.bfloat16), -1, 0, True)
    late_in = [shifted(late_out[0], 0, -1, True), shifted(late_out[1], 0, 1, True)]
    row_in = [shifted(part, 0, step, True) for part, step in zip(row_out, (-1, 1))]
    later_sum = back[7].astype(jnp.float32) + late_in[0].astype(jnp.float32) + late_in[1].astype(jnp.float32)
    from_earlier = shifted(later_sum.astype(jnp.bfloat16), 1, 0, True)
    grad_total = (
        back[4].astype(jnp.float32)
        + row_in[0].astype(jnp.float32)
        + row_in[1].astype(jnp.float32)
        + from_later.astype(jnp.float32)
        + from_earlier.astype(jnp.float32)
    )
    attn_all, grad_tile, grad_total = lax.optimization_barrier((attn_all, grad_tile, grad_total))
    dp_count = lax.axis_size("dp")
    sp_count = lax.axis_size("sp")
    dp_index = lax.axis_index("dp")
    core, high = dp_index % 2, dp_index // 2
    row_block = inner_width // dp_count
    model_width = grad_tile.shape[1]
    col_block = model_width // sp_count
    attn_blocks = attn_all.reshape(tile_tok, dp_count // 2, 2, row_block)
    kept_rows = lax.dynamic_index_in_dim(attn_blocks, core, 2, keepdims=False).reshape(tile_tok, -1)
    sent_rows = lax.dynamic_index_in_dim(attn_blocks, 1 - core, 2, keepdims=False).reshape(tile_tok, -1)
    contract_tokens = (((0,), (0,)), ((), ()))
    kept_part = lax.dot_general(grad_tile, kept_rows, contract_tokens, preferred_element_type=jnp.float32)
    sent_part = lax.dot_general(grad_tile, sent_rows, contract_tokens, preferred_element_type=jnp.float32)
    sibling_part = lax.ppermute(
        sent_part.astype(jnp.bfloat16), "dp", [(index, index ^ 1) for index in range(dp_count)]
    )
    core_sum = (kept_part + sibling_part.astype(jnp.float32)).astype(jnp.bfloat16)
    by_column = lax.all_to_all(
        core_sum.reshape(sp_count, col_block, -1), "sp", 0, 0, tiled=True
    )
    column_sum = by_column.astype(jnp.float32).sum(0).reshape(col_block, dp_count // 2, row_block)
    own_half = lax.dynamic_index_in_dim(column_sum, high, 1, keepdims=False)
    other_half = lax.dynamic_index_in_dim(column_sum, 1 - high, 1, keepdims=False)
    weight_grad = (
        own_half
        + lax.ppermute(other_half, "dp", [(index, (index + 2) % dp_count) for index in range(dp_count)])
    ).T
    grad_kv = grad_total.astype(jnp.bfloat16)
    return (grad_query[None, None], grad_kv[0][None, None], grad_kv[1][None, None], weight_grad)


def solution(mesh):
    in_specs = (
        P("dp", "sp", None, None),
        P("dp", "sp", None, None),
        P("dp", "sp", None, None),
        P("sp", None),
        P("dp", "sp", None, None),
        P(),
    )
    out_specs = (
        P("dp", "sp", None, None),
        P("dp", "sp", None, None),
        P("dp", "sp", None, None),
        P("dp", "sp"),
    )
    return jax.shard_map(body, mesh=mesh, in_specs=in_specs, out_specs=out_specs, check_vma=False)
```

```python
import functools
import math

import jax
import jax.numpy as jnp
from jax import lax
from jax.experimental import pallas as pl
from jax.sharding import PartitionSpec as P

HEAD = 128
H_TILES = 4


def neighbour_shift(value, axis, time_step, height_step, height_tiles, toward):
    count = lax.axis_size(axis)
    time_tiles = count // height_tiles
    offset = time_step * height_tiles + height_step
    pairs = []
    for tile in range(count):
        time_row, height_col = divmod(tile, height_tiles)
        if 0 <= time_row + time_step < time_tiles and 0 <= height_col + height_step < height_tiles:
            pairs.append((tile, tile + offset) if toward else (tile + offset, tile))
    return lax.ppermute(value, axis, pairs)


def tile_attention(mask_ref, query_ref, grad_ref, *refs, score_scale):
    directions = refs[:9]
    attn_ref, dq_ref = refs[9:11]
    out_directions = refs[11:]
    rows_by_rows = (((1,), (1,)), ((), ()))
    cols_by_cols = (((0,), (0,)), ((), ()))
    query = query_ref[...]
    grad = grad_ref[...]
    key = jnp.concatenate([ref[0] for ref in directions], axis=0)
    value = jnp.concatenate([ref[1] for ref in directions], axis=0)
    scores = lax.dot_general(query, key, rows_by_rows, preferred_element_type=jnp.float32) * score_scale
    scores = jnp.where(mask_ref[...] > 0, scores, -1e30)
    row_peak = jnp.max(scores, axis=1, keepdims=True)
    exp_scores = jnp.exp(scores - row_peak)
    probs = exp_scores / jnp.sum(exp_scores, axis=1, keepdims=True)
    probs_low = probs.astype(jnp.bfloat16)
    attn = jnp.dot(probs_low, value, preferred_element_type=jnp.float32).astype(jnp.bfloat16)
    attn_ref[...] = attn
    row_delta = jnp.sum(grad.astype(jnp.float32) * attn.astype(jnp.float32), axis=1, keepdims=True)
    dprobs = lax.dot_general(grad, value, rows_by_rows, preferred_element_type=jnp.float32)
    dscores = (probs * (dprobs - row_delta)).astype(jnp.bfloat16)
    dq_ref[...] = (jnp.dot(dscores, key, preferred_element_type=jnp.float32) * score_scale).astype(jnp.bfloat16)
    grad_key = (
        lax.dot_general(dscores, query, cols_by_cols, preferred_element_type=jnp.float32) * score_scale
    ).astype(jnp.bfloat16)
    grad_value = lax.dot_general(probs_low, grad, cols_by_cols, preferred_element_type=jnp.float32).astype(jnp.bfloat16)
    tile_tok = query.shape[0]
    for number, ref in enumerate(out_directions):
        rows = slice(number * tile_tok, (number + 1) * tile_tok)
        ref[0] = grad_key[rows]
        ref[1] = grad_value[rows]


def body(queries, keys, values, tile_lists, grad_out, w_out):
    query_tile = queries[0, 0]
    key_tile = keys[0, 0]
    value_tile = values[0, 0]
    grad_tile = grad_out[0, 0]
    listed = tile_lists[0]
    tile_tok, inner_width = query_tile.shape
    slot_count = listed.shape[0]
    height_tiles = H_TILES
    score_scale = 1.0 / math.sqrt(HEAD)
    own_tile = lax.axis_index("sp")
    key_value = jnp.stack([key_tile, value_tile])
    def shifted(value, time_step, height_step, toward):
        return neighbour_shift(value, "sp", time_step, height_step, height_tiles, toward)

    earlier, left_own, right_own = lax.optimization_barrier(
        (
            shifted(key_value, -1, 0, False),
            shifted(key_value, 0, -1, False),
            shifted(key_value, 0, 1, False),
        )
    )
    later = shifted(key_value, 1, 0, False)
    gathered = [
        shifted(earlier, 0, -1, False), earlier, shifted(earlier, 0, 1, False),
        left_own, key_value, right_own,
        shifted(later, 0, -1, False), later, shifted(later, 0, 1, False),
    ]
    valid_slot = listed >= 0
    time_gap = listed // height_tiles - own_tile // height_tiles
    height_gap = listed % height_tiles - own_tile % height_tiles
    slot_index = jnp.where(valid_slot, (time_gap + 1) * 3 + height_gap + 1, 4)
    direction_count = 9
    listed_direction = jnp.any(
        (slot_index[:, None] == jnp.arange(direction_count, dtype=jnp.int32)[None, :]) & valid_slot[:, None],
        axis=0,
    )
    key_count = direction_count * tile_tok
    mask_row = jnp.repeat(listed_direction, tile_tok).astype(jnp.int32).reshape(1, key_count)
    grad_attn = lax.dot_general(
        grad_tile, w_out, (((1,), (1,)), ((), ())), preferred_element_type=jnp.float32
    ).astype(jnp.bfloat16)
    head_count = inner_width // HEAD
    tile_spec = pl.BlockSpec((tile_tok, HEAD), lambda head: (0, head))
    single_spec = pl.BlockSpec((2, tile_tok, HEAD), lambda head: (0, 0, head))
    single_shape = jax.ShapeDtypeStruct((2, tile_tok, inner_width), jnp.bfloat16)
    tile_shape = jax.ShapeDtypeStruct((tile_tok, inner_width), jnp.bfloat16)
    outputs = pl.pallas_call(
        functools.partial(tile_attention, score_scale=score_scale),
        grid=(head_count,),
        in_specs=[pl.BlockSpec((1, key_count), lambda head: (0, 0)), tile_spec, tile_spec, *[single_spec] * direction_count],
        out_specs=[tile_spec, tile_spec, *[single_spec] * direction_count],
        out_shape=[tile_shape, tile_shape, *[single_shape] * direction_count],
        cost_estimate=pl.CostEstimate(
            flops=2 * 5 * tile_tok * key_count * inner_width,
            transcendentals=head_count * tile_tok * key_count,
            bytes_accessed=2 * 2 * (2 * tile_tok + 2 * key_count) * inner_width,
        ),
    )(
        mask_row,
        query_tile,
        grad_attn,
        *gathered,
    )
    attn_all, grad_query = outputs[:2]
    back = outputs[2:]
    dp_count = lax.axis_size("dp")
    sp_count = lax.axis_size("sp")
    dp_index = lax.axis_index("dp")
    core, high = dp_index % 2, dp_index // 2
    row_block = inner_width // dp_count
    model_width = grad_tile.shape[1]
    col_block = model_width // sp_count
    attn_blocks = attn_all.reshape(tile_tok, dp_count // 2, 2, row_block)
    kept_rows = lax.dynamic_index_in_dim(attn_blocks, core, 2, keepdims=False).reshape(tile_tok, -1)
    sent_rows = lax.dynamic_index_in_dim(attn_blocks, 1 - core, 2, keepdims=False).reshape(tile_tok, -1)
    contract_tokens = (((0,), (0,)), ((), ()))
    kept_part = lax.dot_general(grad_tile, kept_rows, contract_tokens, preferred_element_type=jnp.float32)
    sent_part = lax.dot_general(grad_tile, sent_rows, contract_tokens, preferred_element_type=jnp.float32)
    sibling_part = lax.ppermute(
        sent_part.astype(jnp.bfloat16), "dp", [(index, index ^ 1) for index in range(dp_count)]
    )
    core_sum = (kept_part + sibling_part.astype(jnp.float32)).reshape(model_width, dp_count // 2, row_block)
    own_half = lax.dynamic_index_in_dim(core_sum, high, 1, keepdims=False)
    other_half = lax.dynamic_index_in_dim(core_sum, 1 - high, 1, keepdims=False).astype(jnp.bfloat16)
    partner_half = lax.ppermute(
        other_half, "dp", [(index, (index + 2) % dp_count) for index in range(dp_count)]
    )
    clip_sum = (own_half + partner_half.astype(jnp.float32)).astype(jnp.bfloat16)
    by_column = lax.all_to_all(clip_sum.reshape(sp_count, col_block, row_block), "sp", 0, 0, tiled=True)
    weight_grad = by_column.astype(jnp.float32).sum(0).T
    early_in = [shifted(back[0], 0, -1, True), shifted(back[2], 0, 1, True)]
    early_in, late_out, row_out = lax.optimization_barrier((early_in, [back[6], back[8]], [back[3], back[5]]))
    earlier_sum = back[1].astype(jnp.float32) + early_in[0].astype(jnp.float32) + early_in[1].astype(jnp.float32)
    from_later = shifted(earlier_sum.astype(jnp.bfloat16), -1, 0, True)
    late_in = [shifted(late_out[0], 0, -1, True), shifted(late_out[1], 0, 1, True)]
    row_in = [shifted(part, 0, step, True) for part, step in zip(row_out, (-1, 1))]
    later_sum = back[7].astype(jnp.float32) + late_in[0].astype(jnp.float32) + late_in[1].astype(jnp.float32)
    from_earlier = shifted(later_sum.astype(jnp.bfloat16), 1, 0, True)
    grad_total = (
        back[4].astype(jnp.float32)
        + row_in[0].astype(jnp.float32)
        + row_in[1].astype(jnp.float32)
        + from_later.astype(jnp.float32)
        + from_earlier.astype(jnp.float32)
    )
    grad_kv = grad_total.astype(jnp.bfloat16)
    return (grad_query[None, None], grad_kv[0][None, None], grad_kv[1][None, None], weight_grad)


def solution(mesh):
    in_specs = (
        P("dp", "sp", None, None),
        P("dp", "sp", None, None),
        P("dp", "sp", None, None),
        P("sp", None),
        P("dp", "sp", None, None),
        P(),
    )
    out_specs = (
        P("dp", "sp", None, None),
        P("dp", "sp", None, None),
        P("dp", "sp", None, None),
        P("dp", "sp"),
    )
    return jax.shard_map(body, mesh=mesh, in_specs=in_specs, out_specs=out_specs, check_vma=False)
```

```python
import functools
import math

import jax
import jax.numpy as jnp
from jax import lax
from jax.experimental import pallas as pl
from jax.sharding import PartitionSpec as P

HEAD = 128
H_TILES = 4


def neighbour_shift(value, axis, time_step, height_step, height_tiles, toward):
    count = lax.axis_size(axis)
    time_tiles = count // height_tiles
    offset = time_step * height_tiles + height_step
    pairs = []
    for tile in range(count):
        time_row, height_col = divmod(tile, height_tiles)
        if 0 <= time_row + time_step < time_tiles and 0 <= height_col + height_step < height_tiles:
            pairs.append((tile, tile + offset) if toward else (tile + offset, tile))
    return lax.ppermute(value, axis, pairs)


def tile_attention(mask_ref, query_ref, grad_ref, *refs, score_scale):
    directions = refs[:9]
    attn_ref, dq_ref = refs[9:11]
    out_directions = refs[11:]
    rows_by_rows = (((1,), (1,)), ((), ()))
    cols_by_cols = (((0,), (0,)), ((), ()))
    query = query_ref[...]
    grad = grad_ref[...]
    key = jnp.concatenate([ref[0] for ref in directions], axis=0)
    value = jnp.concatenate([ref[1] for ref in directions], axis=0)
    scores = lax.dot_general(query, key, rows_by_rows, preferred_element_type=jnp.float32) * score_scale
    scores = jnp.where(mask_ref[...] > 0, scores, -1e30)
    row_peak = jnp.max(scores, axis=1, keepdims=True)
    exp_scores = jnp.exp(scores - row_peak)
    probs = exp_scores * (1.0 / jnp.sum(exp_scores, axis=1, keepdims=True))
    probs_low = probs.astype(jnp.bfloat16)
    attn = jnp.dot(probs_low, value, preferred_element_type=jnp.float32).astype(jnp.bfloat16)
    attn_ref[...] = attn
    row_delta = jnp.sum(grad.astype(jnp.float32) * attn.astype(jnp.float32), axis=1, keepdims=True)
    dprobs = lax.dot_general(grad, value, rows_by_rows, preferred_element_type=jnp.float32)
    dscores = (probs * (dprobs - row_delta)).astype(jnp.bfloat16)
    dq_ref[...] = (jnp.dot(dscores, key, preferred_element_type=jnp.float32) * score_scale).astype(jnp.bfloat16)
    grad_key = (
        lax.dot_general(dscores, query, cols_by_cols, preferred_element_type=jnp.float32) * score_scale
    ).astype(jnp.bfloat16)
    grad_value = lax.dot_general(probs_low, grad, cols_by_cols, preferred_element_type=jnp.float32).astype(jnp.bfloat16)
    tile_tok = query.shape[0]
    for number, ref in enumerate(out_directions):
        rows = slice(number * tile_tok, (number + 1) * tile_tok)
        ref[0] = grad_key[rows]
        ref[1] = grad_value[rows]


def body(queries, keys, values, tile_lists, grad_out, w_out):
    query_tile = queries[0, 0]
    key_tile = keys[0, 0]
    value_tile = values[0, 0]
    grad_tile = grad_out[0, 0]
    listed = tile_lists[0]
    tile_tok, inner_width = query_tile.shape
    slot_count = listed.shape[0]
    height_tiles = H_TILES
    score_scale = 1.0 / math.sqrt(HEAD)
    own_tile = lax.axis_index("sp")
    key_value = jnp.stack([key_tile, value_tile])
    def shifted(value, time_step, height_step, toward):
        return neighbour_shift(value, "sp", time_step, height_step, height_tiles, toward)

    earlier, left_own, right_own = lax.optimization_barrier(
        (
            shifted(key_value, -1, 0, False),
            shifted(key_value, 0, -1, False),
            shifted(key_value, 0, 1, False),
        )
    )
    later = shifted(key_value, 1, 0, False)
    gathered = [
        shifted(earlier, 0, -1, False), earlier, shifted(earlier, 0, 1, False),
        left_own, key_value, right_own,
        shifted(later, 0, -1, False), later, shifted(later, 0, 1, False),
    ]
    valid_slot = listed >= 0
    time_gap = listed // height_tiles - own_tile // height_tiles
    height_gap = listed % height_tiles - own_tile % height_tiles
    slot_index = jnp.where(valid_slot, (time_gap + 1) * 3 + height_gap + 1, 4)
    direction_count = 9
    listed_direction = jnp.any(
        (slot_index[:, None] == jnp.arange(direction_count, dtype=jnp.int32)[None, :]) & valid_slot[:, None],
        axis=0,
    )
    key_count = direction_count * tile_tok
    mask_row = jnp.repeat(listed_direction, tile_tok).astype(jnp.int32).reshape(1, key_count)
    grad_attn = lax.dot_general(
        grad_tile, w_out, (((1,), (1,)), ((), ())), preferred_element_type=jnp.float32
    ).astype(jnp.bfloat16)
    head_count = inner_width // HEAD
    tile_spec = pl.BlockSpec((tile_tok, HEAD), lambda head: (0, head))
    single_spec = pl.BlockSpec((2, tile_tok, HEAD), lambda head: (0, 0, head))
    single_shape = jax.ShapeDtypeStruct((2, tile_tok, inner_width), jnp.bfloat16)
    tile_shape = jax.ShapeDtypeStruct((tile_tok, inner_width), jnp.bfloat16)
    outputs = pl.pallas_call(
        functools.partial(tile_attention, score_scale=score_scale),
        grid=(head_count,),
        in_specs=[pl.BlockSpec((1, key_count), lambda head: (0, 0)), tile_spec, tile_spec, *[single_spec] * direction_count],
        out_specs=[tile_spec, tile_spec, *[single_spec] * direction_count],
        out_shape=[tile_shape, tile_shape, *[single_shape] * direction_count],
        cost_estimate=pl.CostEstimate(
            flops=2 * 5 * tile_tok * key_count * inner_width,
            transcendentals=head_count * tile_tok * key_count,
            bytes_accessed=2 * 2 * (2 * tile_tok + 2 * key_count) * inner_width,
        ),
    )(
        mask_row,
        query_tile,
        grad_attn,
        *gathered,
    )
    attn_all, grad_query = outputs[:2]
    back = outputs[2:]
    dp_count = lax.axis_size("dp")
    sp_count = lax.axis_size("sp")
    dp_index = lax.axis_index("dp")
    core, high = dp_index % 2, dp_index // 2
    row_block = inner_width // dp_count
    model_width = grad_tile.shape[1]
    col_block = model_width // sp_count
    attn_blocks = attn_all.reshape(tile_tok, dp_count // 2, 2, row_block)
    kept_rows = lax.dynamic_index_in_dim(attn_blocks, core, 2, keepdims=False).reshape(tile_tok, -1)
    sent_rows = lax.dynamic_index_in_dim(attn_blocks, 1 - core, 2, keepdims=False).reshape(tile_tok, -1)
    contract_tokens = (((0,), (0,)), ((), ()))
    kept_part = lax.dot_general(grad_tile, kept_rows, contract_tokens, preferred_element_type=jnp.float32)
    sent_part = lax.dot_general(grad_tile, sent_rows, contract_tokens, preferred_element_type=jnp.float32)
    sibling_part = lax.ppermute(
        sent_part.astype(jnp.bfloat16), "dp", [(index, index ^ 1) for index in range(dp_count)]
    )
    core_sum = (kept_part + sibling_part.astype(jnp.float32)).astype(jnp.bfloat16)
    by_column = lax.all_to_all(
        core_sum.reshape(sp_count, col_block, -1), "sp", 0, 0, tiled=True
    )
    column_sum = by_column.astype(jnp.float32).sum(0).reshape(col_block, dp_count // 2, row_block)
    own_half = lax.dynamic_index_in_dim(column_sum, high, 1, keepdims=False)
    other_half = lax.dynamic_index_in_dim(column_sum, 1 - high, 1, keepdims=False)
    weight_grad = (
        own_half
        + lax.ppermute(other_half, "dp", [(index, (index + 2) % dp_count) for index in range(dp_count)])
    ).T
    early_in = [shifted(back[0], 0, -1, True), shifted(back[2], 0, 1, True)]
    early_in, late_out, row_out = lax.optimization_barrier((early_in, [back[6], back[8]], [back[3], back[5]]))
    earlier_sum = back[1].astype(jnp.float32) + early_in[0].astype(jnp.float32) + early_in[1].astype(jnp.float32)
    from_later = shifted(earlier_sum.astype(jnp.bfloat16), -1, 0, True)
    late_in = [shifted(late_out[0], 0, -1, True), shifted(late_out[1], 0, 1, True)]
    row_in = [shifted(part, 0, step, True) for part, step in zip(row_out, (-1, 1))]
    later_sum = back[7].astype(jnp.float32) + late_in[0].astype(jnp.float32) + late_in[1].astype(jnp.float32)
    from_earlier = shifted(later_sum.astype(jnp.bfloat16), 1, 0, True)
    grad_total = (
        back[4].astype(jnp.float32)
        + row_in[0].astype(jnp.float32)
        + row_in[1].astype(jnp.float32)
        + from_later.astype(jnp.float32)
        + from_earlier.astype(jnp.float32)
    )
    grad_kv = grad_total.astype(jnp.bfloat16)
    return (grad_query[None, None], grad_kv[0][None, None], grad_kv[1][None, None], weight_grad)


def solution(mesh):
    in_specs = (
        P("dp", "sp", None, None),
        P("dp", "sp", None, None),
        P("dp", "sp", None, None),
        P("sp", None),
        P("dp", "sp", None, None),
        P(),
    )
    out_specs = (
        P("dp", "sp", None, None),
        P("dp", "sp", None, None),
        P("dp", "sp", None, None),
        P("dp", "sp"),
    )
    return jax.shard_map(body, mesh=mesh, in_specs=in_specs, out_specs=out_specs, check_vma=False)
```

```python
import functools
import math

import jax
import jax.numpy as jnp
from jax import lax
from jax.experimental import pallas as pl
from jax.sharding import PartitionSpec as P

HEAD = 128
H_TILES = 4


def neighbour_shift(value, axis, time_step, height_step, height_tiles, toward):
    count = lax.axis_size(axis)
    time_tiles = count // height_tiles
    offset = time_step * height_tiles + height_step
    pairs = []
    for tile in range(count):
        time_row, height_col = divmod(tile, height_tiles)
        if 0 <= time_row + time_step < time_tiles and 0 <= height_col + height_step < height_tiles:
            pairs.append((tile, tile + offset) if toward else (tile + offset, tile))
    return lax.ppermute(value, axis, pairs)


def tile_attention(mask_ref, query_ref, grad_ref, *refs, score_scale):
    directions = refs[:9]
    attn_ref, dq_ref = refs[9:11]
    out_directions = refs[11:]
    rows_by_rows = (((1,), (1,)), ((), ()))
    cols_by_cols = (((0,), (0,)), ((), ()))
    query = query_ref[...]
    grad = grad_ref[...]
    key = jnp.concatenate([ref[0] for ref in directions], axis=0)
    value = jnp.concatenate([ref[1] for ref in directions], axis=0)
    scores = lax.dot_general(query, key, rows_by_rows, preferred_element_type=jnp.float32) * score_scale
    scores = jnp.where(mask_ref[...] > 0, scores, -1e30)
    row_peak = jnp.max(scores, axis=1, keepdims=True)
    exp_scores = jnp.exp(scores - row_peak)
    probs = exp_scores * (1.0 / jnp.sum(exp_scores, axis=1, keepdims=True))
    probs_low = probs.astype(jnp.bfloat16)
    attn = jnp.dot(probs_low, value, preferred_element_type=jnp.float32).astype(jnp.bfloat16)
    attn_ref[...] = attn
    row_delta = jnp.sum(grad.astype(jnp.float32) * attn.astype(jnp.float32), axis=1, keepdims=True)
    dprobs = lax.dot_general(grad, value, rows_by_rows, preferred_element_type=jnp.float32)
    dscores = (probs * (dprobs - row_delta)).astype(jnp.bfloat16)
    dq_ref[...] = (jnp.dot(dscores, key, preferred_element_type=jnp.float32) * score_scale).astype(jnp.bfloat16)
    grad_key = (
        lax.dot_general(dscores, query, cols_by_cols, preferred_element_type=jnp.float32) * score_scale
    ).astype(jnp.bfloat16)
    grad_value = lax.dot_general(probs_low, grad, cols_by_cols, preferred_element_type=jnp.float32).astype(jnp.bfloat16)
    tile_tok = query.shape[0]
    for number, ref in enumerate(out_directions):
        rows = slice(number * tile_tok, (number + 1) * tile_tok)
        ref[0] = grad_key[rows]
        ref[1] = grad_value[rows]


def body(queries, keys, values, tile_lists, grad_out, w_out):
    query_tile = queries[0, 0]
    key_tile = keys[0, 0]
    value_tile = values[0, 0]
    grad_tile = grad_out[0, 0]
    listed = tile_lists[0]
    tile_tok, inner_width = query_tile.shape
    slot_count = listed.shape[0]
    height_tiles = H_TILES
    score_scale = 1.0 / math.sqrt(HEAD)
    own_tile = lax.axis_index("sp")
    key_value = jnp.stack([key_tile, value_tile])
    def shifted(value, time_step, height_step, toward):
        return neighbour_shift(value, "sp", time_step, height_step, height_tiles, toward)

    earlier, left_own, right_own = lax.optimization_barrier(
        (
            shifted(key_value, -1, 0, False),
            shifted(key_value, 0, -1, False),
            shifted(key_value, 0, 1, False),
        )
    )
    later = shifted(key_value, 1, 0, False)
    gathered = [
        shifted(earlier, 0, -1, False), earlier, shifted(earlier, 0, 1, False),
        left_own, key_value, right_own,
        shifted(later, 0, -1, False), later, shifted(later, 0, 1, False),
    ]
    valid_slot = listed >= 0
    time_gap = listed // height_tiles - own_tile // height_tiles
    height_gap = listed % height_tiles - own_tile % height_tiles
    slot_index = jnp.where(valid_slot, (time_gap + 1) * 3 + height_gap + 1, 4)
    direction_count = 9
    listed_direction = jnp.any(
        (slot_index[:, None] == jnp.arange(direction_count, dtype=jnp.int32)[None, :]) & valid_slot[:, None],
        axis=0,
    )
    key_count = direction_count * tile_tok
    mask_row = jnp.repeat(listed_direction, tile_tok).astype(jnp.int32).reshape(1, key_count)
    grad_attn = lax.dot_general(
        grad_tile, w_out, (((1,), (1,)), ((), ())), preferred_element_type=jnp.float32
    ).astype(jnp.bfloat16)
    head_count = inner_width // HEAD
    tile_spec = pl.BlockSpec((tile_tok, HEAD), lambda head: (0, head))
    single_spec = pl.BlockSpec((2, tile_tok, HEAD), lambda head: (0, 0, head))
    single_shape = jax.ShapeDtypeStruct((2, tile_tok, inner_width), jnp.bfloat16)
    tile_shape = jax.ShapeDtypeStruct((tile_tok, inner_width), jnp.bfloat16)
    outputs = pl.pallas_call(
        functools.partial(tile_attention, score_scale=score_scale),
        grid=(head_count,),
        in_specs=[pl.BlockSpec((1, key_count), lambda head: (0, 0)), tile_spec, tile_spec, *[single_spec] * direction_count],
        out_specs=[tile_spec, tile_spec, *[single_spec] * direction_count],
        out_shape=[tile_shape, tile_shape, *[single_shape] * direction_count],
        cost_estimate=pl.CostEstimate(
            flops=2 * 5 * tile_tok * key_count * inner_width,
            transcendentals=head_count * tile_tok * key_count,
            bytes_accessed=2 * 2 * (2 * tile_tok + 2 * key_count) * inner_width,
        ),
    )(
        mask_row,
        query_tile,
        grad_attn,
        *gathered,
    )
    attn_all, grad_query = outputs[:2]
    back = outputs[2:]
    dp_count = lax.axis_size("dp")
    sp_count = lax.axis_size("sp")
    dp_index = lax.axis_index("dp")
    core, high = dp_index % 2, dp_index // 2
    row_block = inner_width // dp_count
    model_width = grad_tile.shape[1]
    col_block = model_width // sp_count
    attn_blocks = attn_all.reshape(tile_tok, dp_count // 2, 2, row_block)
    kept_rows = lax.dynamic_index_in_dim(attn_blocks, core, 2, keepdims=False).reshape(tile_tok, -1)
    sent_rows = lax.dynamic_index_in_dim(attn_blocks, 1 - core, 2, keepdims=False).reshape(tile_tok, -1)
    contract_tokens = (((0,), (0,)), ((), ()))
    kept_part = lax.dot_general(grad_tile, kept_rows, contract_tokens, preferred_element_type=jnp.float32)
    sent_part = lax.dot_general(grad_tile, sent_rows, contract_tokens, preferred_element_type=jnp.float32)
    sibling_part = lax.ppermute(
        sent_part.astype(jnp.bfloat16), "dp", [(index, index ^ 1) for index in range(dp_count)]
    )
    core_sum = (kept_part + sibling_part.astype(jnp.float32)).astype(jnp.bfloat16)
    early_in = [shifted(back[0], 0, -1, True), shifted(back[2], 0, 1, True)]
    early_in, late_out, row_out, core_sum = lax.optimization_barrier(
        (early_in, [back[6], back[8]], [back[3], back[5]], core_sum)
    )
    by_column = lax.all_to_all(
        core_sum.reshape(sp_count, col_block, -1), "sp", 0, 0, tiled=True
    )
    column_sum = by_column.astype(jnp.float32).sum(0).reshape(col_block, dp_count // 2, row_block)
    own_half = lax.dynamic_index_in_dim(column_sum, high, 1, keepdims=False)
    other_half = lax.dynamic_index_in_dim(column_sum, 1 - high, 1, keepdims=False)
    weight_grad = (
        own_half
        + lax.ppermute(other_half, "dp", [(index, (index + 2) % dp_count) for index in range(dp_count)])
    ).T
    earlier_sum = back[1].astype(jnp.float32) + early_in[0].astype(jnp.float32) + early_in[1].astype(jnp.float32)
    from_later = shifted(earlier_sum.astype(jnp.bfloat16), -1, 0, True)
    late_in = [shifted(late_out[0], 0, -1, True), shifted(late_out[1], 0, 1, True)]
    row_in = [shifted(part, 0, step, True) for part, step in zip(row_out, (-1, 1))]
    later_sum = back[7].astype(jnp.float32) + late_in[0].astype(jnp.float32) + late_in[1].astype(jnp.float32)
    from_earlier = shifted(later_sum.astype(jnp.bfloat16), 1, 0, True)
    grad_total = (
        back[4].astype(jnp.float32)
        + row_in[0].astype(jnp.float32)
        + row_in[1].astype(jnp.float32)
        + from_later.astype(jnp.float32)
        + from_earlier.astype(jnp.float32)
    )
    grad_kv = grad_total.astype(jnp.bfloat16)
    return (grad_query[None, None], grad_kv[0][None, None], grad_kv[1][None, None], weight_grad)


def solution(mesh):
    in_specs = (
        P("dp", "sp", None, None),
        P("dp", "sp", None, None),
        P("dp", "sp", None, None),
        P("sp", None),
        P("dp", "sp", None, None),
        P(),
    )
    out_specs = (
        P("dp", "sp", None, None),
        P("dp", "sp", None, None),
        P("dp", "sp", None, None),
        P("dp", "sp"),
    )
    return jax.shard_map(body, mesh=mesh, in_specs=in_specs, out_specs=out_specs, check_vma=False)
```

```python
import functools
import math

import jax
import jax.numpy as jnp
from jax import lax
from jax.experimental import pallas as pl
from jax.sharding import PartitionSpec as P

HEAD = 128
H_TILES = 4


def neighbour_shift(value, axis, time_step, height_step, height_tiles, toward):
    count = lax.axis_size(axis)
    time_tiles = count // height_tiles
    offset = time_step * height_tiles + height_step
    pairs = []
    for tile in range(count):
        time_row, height_col = divmod(tile, height_tiles)
        if 0 <= time_row + time_step < time_tiles and 0 <= height_col + height_step < height_tiles:
            pairs.append((tile, tile + offset) if toward else (tile + offset, tile))
    return lax.ppermute(value, axis, pairs)


def tile_attention(mask_ref, query_ref, grad_ref, *refs, score_scale):
    directions = refs[:9]
    attn_ref, dq_ref = refs[9:11]
    out_directions = refs[11:]
    rows_by_rows = (((1,), (1,)), ((), ()))
    cols_by_cols = (((0,), (0,)), ((), ()))
    query = query_ref[...]
    grad = grad_ref[...]
    key = jnp.concatenate([ref[0] for ref in directions], axis=0)
    value = jnp.concatenate([ref[1] for ref in directions], axis=0)
    scores = lax.dot_general(query, key, rows_by_rows, preferred_element_type=jnp.float32) * score_scale
    scores = jnp.where(mask_ref[...] > 0, scores, -1e30)
    row_peak = jnp.max(scores, axis=1, keepdims=True)
    exp_scores = jnp.exp(scores - row_peak)
    probs = exp_scores * (1.0 / jnp.sum(exp_scores, axis=1, keepdims=True))
    probs_low = probs.astype(jnp.bfloat16)
    attn = jnp.dot(probs_low, value, preferred_element_type=jnp.float32).astype(jnp.bfloat16)
    attn_ref[...] = attn
    row_delta = jnp.sum(grad.astype(jnp.float32) * attn.astype(jnp.float32), axis=1, keepdims=True)
    dprobs = lax.dot_general(grad, value, rows_by_rows, preferred_element_type=jnp.float32)
    dscores = (probs * (dprobs - row_delta)).astype(jnp.bfloat16)
    dq_ref[...] = (jnp.dot(dscores, key, preferred_element_type=jnp.float32) * score_scale).astype(jnp.bfloat16)
    grad_key = (
        lax.dot_general(dscores, query, cols_by_cols, preferred_element_type=jnp.float32) * score_scale
    ).astype(jnp.bfloat16)
    grad_value = lax.dot_general(probs_low, grad, cols_by_cols, preferred_element_type=jnp.float32).astype(jnp.bfloat16)
    tile_tok = query.shape[0]
    for number, ref in enumerate(out_directions):
        rows = slice(number * tile_tok, (number + 1) * tile_tok)
        ref[0] = grad_key[rows]
        ref[1] = grad_value[rows]


def body(queries, keys, values, tile_lists, grad_out, w_out):
    query_tile = queries[0, 0]
    key_tile = keys[0, 0]
    value_tile = values[0, 0]
    grad_tile = grad_out[0, 0]
    listed = tile_lists[0]
    tile_tok, inner_width = query_tile.shape
    slot_count = listed.shape[0]
    height_tiles = H_TILES
    score_scale = 1.0 / math.sqrt(HEAD)
    own_tile = lax.axis_index("sp")
    key_value = jnp.stack([key_tile, value_tile])
    def shifted(value, time_step, height_step, toward):
        return neighbour_shift(value, "sp", time_step, height_step, height_tiles, toward)

    earlier, left_own, right_own = lax.optimization_barrier(
        (
            shifted(key_value, -1, 0, False),
            shifted(key_value, 0, -1, False),
            shifted(key_value, 0, 1, False),
        )
    )
    later = shifted(key_value, 1, 0, False)
    gathered = [
        shifted(earlier, 0, -1, False), earlier, shifted(earlier, 0, 1, False),
        left_own, key_value, right_own,
        shifted(later, 0, -1, False), later, shifted(later, 0, 1, False),
    ]
    valid_slot = listed >= 0
    time_gap = listed // height_tiles - own_tile // height_tiles
    height_gap = listed % height_tiles - own_tile % height_tiles
    slot_index = jnp.where(valid_slot, (time_gap + 1) * 3 + height_gap + 1, 4)
    direction_count = 9
    listed_direction = jnp.any(
        (slot_index[:, None] == jnp.arange(direction_count, dtype=jnp.int32)[None, :]) & valid_slot[:, None],
        axis=0,
    )
    key_count = direction_count * tile_tok
    mask_row = jnp.repeat(listed_direction, tile_tok).astype(jnp.int32).reshape(1, key_count)
    grad_attn = lax.dot_general(
        grad_tile, w_out, (((1,), (1,)), ((), ())), preferred_element_type=jnp.float32
    ).astype(jnp.bfloat16)
    head_count = inner_width // HEAD
    tile_spec = pl.BlockSpec((tile_tok, HEAD), lambda head: (0, head))
    single_spec = pl.BlockSpec((2, tile_tok, HEAD), lambda head: (0, 0, head))
    single_shape = jax.ShapeDtypeStruct((2, tile_tok, inner_width), jnp.bfloat16)
    tile_shape = jax.ShapeDtypeStruct((tile_tok, inner_width), jnp.bfloat16)
    outputs = pl.pallas_call(
        functools.partial(tile_attention, score_scale=score_scale),
        grid=(head_count,),
        in_specs=[pl.BlockSpec((1, key_count), lambda head: (0, 0)), tile_spec, tile_spec, *[single_spec] * direction_count],
        out_specs=[tile_spec, tile_spec, *[single_spec] * direction_count],
        out_shape=[tile_shape, tile_shape, *[single_shape] * direction_count],
        cost_estimate=pl.CostEstimate(
            flops=2 * 5 * tile_tok * key_count * inner_width,
            transcendentals=head_count * tile_tok * key_count,
            bytes_accessed=2 * 2 * (2 * tile_tok + 2 * key_count) * inner_width,
        ),
    )(
        mask_row,
        query_tile,
        grad_attn,
        *gathered,
    )
    attn_all, grad_query = outputs[:2]
    back = outputs[2:]
    dp_count = lax.axis_size("dp")
    sp_count = lax.axis_size("sp")
    dp_index = lax.axis_index("dp")
    core, high = dp_index % 2, dp_index // 2
    row_block = inner_width // dp_count
    model_width = grad_tile.shape[1]
    col_block = model_width // sp_count
    attn_blocks = attn_all.reshape(tile_tok, dp_count // 2, 2, row_block)
    kept_rows = lax.dynamic_index_in_dim(attn_blocks, core, 2, keepdims=False).reshape(tile_tok, -1)
    sent_rows = lax.dynamic_index_in_dim(attn_blocks, 1 - core, 2, keepdims=False).reshape(tile_tok, -1)
    contract_tokens = (((0,), (0,)), ((), ()))
    kept_part = lax.dot_general(grad_tile, kept_rows, contract_tokens, preferred_element_type=jnp.float32)
    sent_part = lax.dot_general(grad_tile, sent_rows, contract_tokens, preferred_element_type=jnp.float32)
    sibling_part = lax.ppermute(
        sent_part.astype(jnp.bfloat16), "dp", [(index, index ^ 1) for index in range(dp_count)]
    )
    core_sum = (kept_part + sibling_part.astype(jnp.float32)).astype(jnp.bfloat16)
    by_column = lax.all_to_all(
        core_sum.reshape(sp_count, col_block, -1), "sp", 0, 0, tiled=True
    )
    column_sum = by_column.astype(jnp.float32).sum(0).reshape(col_block, dp_count // 2, row_block)
    own_half = lax.dynamic_index_in_dim(column_sum, high, 1, keepdims=False)
    other_half = lax.dynamic_index_in_dim(column_sum, 1 - high, 1, keepdims=False)
    weight_grad = (
        own_half
        + lax.ppermute(other_half, "dp", [(index, (index + 2) % dp_count) for index in range(dp_count)])
    ).T
    early_in = [shifted(back[0], 0, -1, True), shifted(back[2], 0, 1, True)]
    early_in, late_out = lax.optimization_barrier((early_in, [back[6], back[8]]))
    earlier_sum = back[1].astype(jnp.float32) + early_in[0].astype(jnp.float32) + early_in[1].astype(jnp.float32)
    from_later = shifted(earlier_sum.astype(jnp.bfloat16), -1, 0, True)
    late_in = [shifted(late_out[0], 0, -1, True), shifted(late_out[1], 0, 1, True)]
    late_in, row_out = lax.optimization_barrier((late_in, [back[3], back[5]]))
    row_in = [shifted(part, 0, step, True) for part, step in zip(row_out, (-1, 1))]
    later_sum = back[7].astype(jnp.float32) + late_in[0].astype(jnp.float32) + late_in[1].astype(jnp.float32)
    from_earlier = shifted(later_sum.astype(jnp.bfloat16), 1, 0, True)
    grad_total = (
        back[4].astype(jnp.float32)
        + row_in[0].astype(jnp.float32)
        + row_in[1].astype(jnp.float32)
        + from_later.astype(jnp.float32)
        + from_earlier.astype(jnp.float32)
    )
    grad_kv = grad_total.astype(jnp.bfloat16)
    return (grad_query[None, None], grad_kv[0][None, None], grad_kv[1][None, None], weight_grad)


def solution(mesh):
    in_specs = (
        P("dp", "sp", None, None),
        P("dp", "sp", None, None),
        P("dp", "sp", None, None),
        P("sp", None),
        P("dp", "sp", None, None),
        P(),
    )
    out_specs = (
        P("dp", "sp", None, None),
        P("dp", "sp", None, None),
        P("dp", "sp", None, None),
        P("dp", "sp"),
    )
    return jax.shard_map(body, mesh=mesh, in_specs=in_specs, out_specs=out_specs, check_vma=False)
```
